512 devices in a mesh: dom: 64 (over z, y), tile: 8 (over x, core).
Axes of the slice: x: 4, y: 8, z: 8, core: 2. Of those that a mesh axis runs over, the one named last changes fastest.
Arguments:
- geometry: float32 [5, 1572864], P(None, 'dom'), may hold values from -4 to 1056, as said below
- opacity: float32 [1572864], P('dom'), may hold values from -7 to -2.5
- colours: float32 [3, 1572864], P(None, 'dom'), may hold values from -6 to 6
- coverage: int32 [64, 8, 12], P('dom', 'tile'), may hold values from -1 to 127, as said below
- gauss_lists: int32 [64, 8, 12, 256], P('dom', 'tile'), may hold values from -1 to 24575, as said below
- orders: int32 [1024, 64], P(('dom', 'tile')), may hold values from 0 to 63, each once within a row
- cotangent: float32 [3, 1024, 256], P(None, ('dom', 'tile')), may hold values from -6 to 6
Outputs:
- rendered: float32 [3, 1024, 256], P(None, ('dom', 'tile'))
- grad_geometry: float32 [5, 1572864], P(None, ('dom', 'tile'))
- grad_opacity: float32 [1572864], P(('dom', 'tile'))
- grad_colours: float32 [3, 1572864], P(None, ('dom', 'tile'))
The draws below stay inside these ranges and needn't reach their ends.
Inputs may be any that keep to these rules, and one draw needn't show every extreme that they name: `geometry`: Rows: centre x and y, two log standard deviations, angle. `coverage`: partition d covers the same number of tiles, 1 to 12, in every group; covered tiles of a group come first in increasing order, at most one in each block of 2 tiles, then -1; exactly one partition covers 12 tiles in every group. `gauss_lists`: A covered slot lists 1 to 256 Gaussians of the partition front to back, then -1; every device has a slot with exactly 256; an uncovered slot holds only -1; a Gaussian appears at most once in its partition. `orders`: each tile's row is a permutation of the partitions.
All inputs are finite; a program needn't handle non-finite values.
Results may differ from the reference program's by a relative error of at most 0.0003.
Values sent between devices are 32-bit elements; how exact they have to be, the bound alone decides.
No kernel may reach another device: no remote copies, remote signals or barrier semaphores. Data moves between devices by JAX's collectives and lax.ppermute only.
A program may use at most 128 MiB of HBM per device.

```python
import math
import jax
import jax.numpy as jnp
from jax import lax

TPD = 2
TSIDE = 16
SLOTS = 256
PIX = 256
PARTS_SIZE = 64
GROUPS = 8
COVMAX = 12
TPG = 128
TILES = 1024
G_PART = 24576
GAUSSIANS = 1572864


def layout(key):
    streams = jax.random.split(jax.random.fold_in(key, 4099), 8)
    most_blocks = COVMAX
    busiest = jax.random.randint(streams[0], (), 0, PARTS_SIZE)
    amount = jax.random.randint(streams[1], (PARTS_SIZE,), max(1, most_blocks // 6), most_blocks // 2 + 1)
    amount = jnp.where(jnp.arange(PARTS_SIZE) == busiest, most_blocks, amount)
    scores = jax.random.randint(streams[3], (PARTS_SIZE, GROUPS, PARTS_SIZE), 0, 1 << 20) * PARTS_SIZE + jnp.arange(PARTS_SIZE)
    shuffled = jnp.argsort(scores, axis=2)
    chosen = shuffled[:, :, :most_blocks]
    slot_index = jnp.arange(most_blocks)
    live_slot = slot_index[None, None, :] < amount[:, None, None]
    keyed = jnp.sort(jnp.where(live_slot, chosen, PARTS_SIZE + chosen), axis=2)
    blocks = keyed % PARTS_SIZE
    offset = jax.random.randint(streams[4], (PARTS_SIZE, GROUPS, most_blocks), 0, TPD)
    tile_all = blocks * TPD + offset
    coverage = jnp.where(live_slot, tile_all, -1)
    counts = jax.random.randint(streams[5], (PARTS_SIZE, GROUPS, most_blocks), 1, SLOTS + 1)
    full_at = jax.random.randint(streams[6], (PARTS_SIZE, GROUPS), 0, 1 << 20) % amount[:, None]
    counts = jnp.where(slot_index[None, None, :] == full_at[:, :, None], SLOTS, counts)
    counts = jnp.where(live_slot, counts, 0)
    shuffle_ids = jax.vmap(lambda part_key: jax.random.permutation(part_key, G_PART))(jax.random.split(streams[7], PARTS_SIZE))
    reserved = (jnp.arange(GROUPS)[:, None, None] * most_blocks + slot_index[None, :, None]) * SLOTS + jnp.arange(SLOTS)[None, None, :]
    gauss_ids = jnp.take(shuffle_ids, reserved.reshape(-1), axis=1).reshape(PARTS_SIZE, GROUPS, most_blocks, SLOTS)
    gauss_lists = jnp.where(jnp.arange(SLOTS)[None, None, None, :] < counts[..., None], gauss_ids, -1)
    return (coverage.astype(jnp.int32), gauss_lists.astype(jnp.int32), tile_all, shuffle_ids)


def draw_coverage(key, part):
    return layout(key)[0]


def draw_gauss_lists(key, part):
    return layout(key)[1]


def draw_geometry(key, part):
    coverage, gauss_lists, tile_all, shuffle_ids = layout(key)
    inverse = jnp.argsort(shuffle_ids, axis=1)
    group_of = inverse // (COVMAX * SLOTS)
    slot_of = inverse // SLOTS % COVMAX
    flat_tiles = tile_all.reshape(PARTS_SIZE, GROUPS * COVMAX)
    home = jnp.take_along_axis(flat_tiles, group_of * COVMAX + slot_of, axis=1)
    row_pos = (home // TPD).astype(jnp.float32)
    col_pos = (group_of * TPD + home % TPD).astype(jnp.float32)
    streams = jax.random.split(jax.random.fold_in(key, 77), 3)
    inside = jnp.clip(0.5 + 0.3 * jax.random.normal(streams[0], (2, PARTS_SIZE, G_PART), jnp.float32), -0.1, 1.1)
    log_scale = jax.random.uniform(streams[1], (2, PARTS_SIZE, G_PART), jnp.float32, math.log(0.08), math.log(0.4))
    centre_x = (col_pos + inside[0]) * TSIDE
    centre_y = (row_pos + inside[1]) * TSIDE
    log_sd = log_scale + math.log(TSIDE)
    angle = jax.random.uniform(streams[2], (PARTS_SIZE, G_PART), jnp.float32, -math.pi, math.pi)
    stacked = jnp.stack([centre_x, centre_y, log_sd[0], log_sd[1], angle], axis=0)
    return stacked.reshape(5, GAUSSIANS).astype(jnp.float32)


def shard_levels(own_key, shape, cuts, low, largest):
    level = 1.0
    for axis_at, blocks in cuts:
        draws = jax.random.uniform(jax.random.fold_in(jax.random.fold_in(own_key, 6), axis_at), (blocks,), jnp.float32, low / len(cuts), largest / len(cuts))
        level = level * jnp.repeat(jnp.exp(draws), shape[axis_at] // blocks).reshape((-1,) + (1,) * (len(shape) - 1 - axis_at))
    return level


def normal_values(stream_key, shape, spread, bound, cuts=(), kind=jnp.bfloat16):
    values = spread * jax.random.normal(stream_key, shape, jnp.float32)
    if cuts:
        values = values * shard_levels(stream_key, shape, cuts, -0.22, 0.18)
    return jnp.clip(values, -bound, bound).astype(kind)


def setup_inputs(seed: int = 0) -> dict:
    splits = jax.random.split(jax.random.key(seed), 8)
    geometry = draw_geometry(jax.random.fold_in(splits[7], 71), 0)
    opacity = jnp.clip(-7.0 + 4.5 * jax.random.uniform(splits[1], (GAUSSIANS,), jnp.float32) ** shard_levels(splits[1], (GAUSSIANS,), ((0, 64),), -0.2, 0.2), -7.0, -2.5)
    colours = normal_values(splits[2], (3, GAUSSIANS), 1.0, 6.0, ((1, 64),), jnp.float32)
    coverage = draw_coverage(jax.random.fold_in(splits[7], 71), 0)
    gauss_lists = draw_gauss_lists(jax.random.fold_in(splits[7], 71), 0)
    orders = jax.vmap(lambda own: jax.random.permutation(own, PARTS_SIZE))(jax.random.split(splits[5], TILES)).reshape((TILES, PARTS_SIZE)).astype(jnp.int32)
    cotangent = normal_values(splits[6], (3, TILES, PIX), 1.0, 6.0, ((1, 512),), jnp.float32)
    return dict(geometry=geometry, opacity=opacity, colours=colours, coverage=coverage, gauss_lists=gauss_lists, orders=orders, cotangent=cotangent)


def blank_tile():
    return jnp.concatenate([jnp.zeros((3, PIX), jnp.float32), jnp.ones((1, PIX), jnp.float32)], axis=0)

def render_tiles(params, pixel_x, pixel_y, live_mask):
    centre_x = params[0][:, None, :]
    centre_y = params[1][:, None, :]
    inv_one = jnp.exp(-2.0 * params[2])
    inv_two = jnp.exp(-2.0 * params[3])
    cosine = jnp.cos(params[4])
    sine_angle = jnp.sin(params[4])
    coef_a = (cosine * cosine * inv_one + sine_angle * sine_angle * inv_two)[:, None, :]
    coef_b = (cosine * sine_angle * (inv_one - inv_two))[:, None, :]
    coef_c = (sine_angle * sine_angle * inv_one + cosine * cosine * inv_two)[:, None, :]
    delta_x = pixel_x[:, :, None] - centre_x
    delta_y = pixel_y[:, :, None] - centre_y
    quadratic = coef_a * delta_x * delta_x + 2.0 * coef_b * delta_x * delta_y + coef_c * delta_y * delta_y
    strength = jax.nn.sigmoid(params[5]) * live_mask
    opaque_part = strength[:, None, :] * jnp.exp(-0.5 * quadratic)
    log_keep = jnp.log1p(-opaque_part)
    running = jnp.cumsum(log_keep, axis=2)
    before = jnp.concatenate([jnp.zeros_like(running[:, :, :1]), running[:, :, :-1]], axis=2)
    weight = opaque_part * jnp.exp(before)
    colour = jnp.einsum('kpg,ckg->kcp', weight, params[6:9], precision=lax.Precision.HIGHEST)
    transmit = jnp.exp(lax.optimization_barrier(jnp.sum(log_keep, axis=2)))
    return (colour, transmit)

def pixel_grid(tile_ids, group_index):
    safe_ids = jnp.maximum(tile_ids, 0)
    block_row = safe_ids // TPD
    column = group_index * TPD + safe_ids % TPD
    within = jnp.arange(PIX, dtype=jnp.int32)
    pixel_x = (column[:, None] * TSIDE + within[None, :] % TSIDE).astype(jnp.float32) + 0.5
    pixel_y = (block_row[:, None] * TSIDE + within[None, :] // TSIDE).astype(jnp.float32) + 0.5
    return (pixel_x, pixel_y)

def part_partials(item):
    params, cover_part, lists_part = item

    def one_group(group_index, tile_ids, entries):
        pixel_x, pixel_y = pixel_grid(tile_ids, group_index)
        live = entries >= 0
        chosen = jnp.take(params, jnp.where(live, entries, 0), axis=1)
        colour, transmit = render_tiles(chosen, pixel_x, pixel_y, live.astype(jnp.float32))
        packed = jnp.concatenate([colour, transmit[:, None, :]], axis=1)
        return jnp.where((tile_ids >= 0)[:, None, None], packed, blank_tile()[None])
    return jax.vmap(one_group)(jnp.arange(GROUPS, dtype=jnp.int32), cover_part, lists_part)

def row_image(item):
    flat_rows, row_table, row_orders = item
    pieces = jnp.take(flat_rows, row_table, axis=0)
    depth = jnp.argsort(row_orders, axis=1).astype(jnp.int32)
    ordered = jnp.take_along_axis(pieces, depth[:, :, None, None], axis=1)
    transmit = ordered[:, :, 3]
    running = jnp.cumprod(transmit, axis=1)
    prefix = jnp.concatenate([jnp.ones_like(running[:, :1]), running[:, :-1]], axis=1)
    return lax.optimization_barrier(jnp.sum(prefix[:, :, None, :] * ordered[:, :, :3], axis=1))

def reference(geometry, opacity, colours, coverage, gauss_lists, orders, cotangent):
    part_index = jnp.arange(PARTS_SIZE, dtype=jnp.int32)[:, None, None]
    group_idx = jnp.arange(GROUPS, dtype=jnp.int32)[None, :, None]
    slot_index = jnp.arange(COVMAX, dtype=jnp.int32)[None, None, :]
    flat_index = (part_index * GROUPS + group_idx) * COVMAX + slot_index
    target = jnp.where(coverage >= 0, coverage, TPG).astype(jnp.int32)
    part_b = jnp.broadcast_to(part_index, coverage.shape)
    group_b = jnp.broadcast_to(group_idx, coverage.shape)
    table = jnp.full((PARTS_SIZE, GROUPS, TPG), PARTS_SIZE * GROUPS * COVMAX, jnp.int32)
    table = table.at[part_b, group_b, target].set(flat_index.astype(jnp.int32), mode='drop')
    table = table.reshape(PARTS_SIZE, GROUPS, PARTS_SIZE, TPD).transpose(2, 1, 3, 0).reshape(PARTS_SIZE, GROUPS * TPD, PARTS_SIZE)
    orders_rows = orders.reshape(PARTS_SIZE, GROUPS * TPD, PARTS_SIZE)

    def forward(geometry, opacity, colours):
        params = jnp.concatenate([geometry, opacity[None, :], colours], axis=0)
        per_part = params.reshape(9, PARTS_SIZE, G_PART).transpose(1, 0, 2)
        partials = lax.map(jax.checkpoint(part_partials), (per_part, coverage, gauss_lists))
        flat_rows = jnp.concatenate([partials.reshape(-1, 4, PIX), blank_tile()[None]], axis=0)
        rows = lax.map(jax.checkpoint(lambda pair: row_image((flat_rows, pair[0], pair[1]))), (table, orders_rows))
        return rows.reshape(TILES, 3, PIX).transpose(1, 0, 2)
    rendered, pullback = jax.vjp(forward, geometry, opacity, colours)
    grads = pullback(cotangent)
    return (rendered, grads[0], grads[1], grads[2])
```

```python
import math

import jax
import jax.numpy as jnp
from jax import lax
from jax.sharding import PartitionSpec as P

TSIDE = 16


def render(params, pixel_x, pixel_y, live_mask):
    centre_x = params[0][:, None, :]
    centre_y = params[1][:, None, :]
    inv_one = jnp.exp(-2.0 * params[2])
    inv_two = jnp.exp(-2.0 * params[3])
    cosine = jnp.cos(params[4])
    sine_angle = jnp.sin(params[4])
    coef_a = (cosine * cosine * inv_one + sine_angle * sine_angle * inv_two)[:, None, :]
    coef_b = (cosine * sine_angle * (inv_one - inv_two))[:, None, :]
    coef_c = (sine_angle * sine_angle * inv_one + cosine * cosine * inv_two)[:, None, :]
    delta_x = pixel_x[:, :, None] - centre_x
    delta_y = pixel_y[:, :, None] - centre_y
    quadratic = (
        coef_a * delta_x * delta_x + 2.0 * coef_b * delta_x * delta_y + coef_c * delta_y * delta_y
    )
    strength = jax.nn.sigmoid(params[5]) * live_mask
    opaque_part = strength[:, None, :] * jnp.exp(-0.5 * quadratic)
    log_keep = jnp.log1p(-opaque_part)
    running = jnp.cumsum(log_keep, axis=2)
    before = jnp.concatenate([jnp.zeros_like(running[:, :, :1]), running[:, :, :-1]], axis=2)
    weight = opaque_part * jnp.exp(before)
    colour = jnp.einsum("kpg,ckg->kcp", weight, params[6:9], precision=lax.Precision.HIGHEST)
    transmit = jnp.exp(jnp.sum(log_keep, axis=2))
    return (colour, transmit)


def pixel_grid(tile_ids, group_index, tiles_per, pixels):
    safe_ids = jnp.maximum(tile_ids, 0)
    block_row = safe_ids // tiles_per
    column = group_index * tiles_per + safe_ids % tiles_per
    within = jnp.arange(pixels, dtype=jnp.int32)
    pixel_x = (column[:, None] * TSIDE + within[None, :] % TSIDE).astype(jnp.float32) + 0.5
    pixel_y = (block_row[:, None] * TSIDE + within[None, :] // TSIDE).astype(jnp.float32) + 0.5
    return (pixel_x, pixel_y)


def composite(arrived, orders, cotangent):
    parts_count = arrived.shape[0]
    ranks_onehot = (
        orders[:, None, :] == jnp.arange(parts_count, dtype=jnp.int32)[None, :, None]
    ).astype(jnp.float32)
    ordered = jnp.einsum("irk,kicp->ircp", ranks_onehot, arrived, precision=lax.Precision.HIGHEST)
    colour = ordered[:, :, :3]
    transmit = ordered[:, :, 3]
    running = jnp.cumprod(transmit, axis=1)
    prefix = jnp.concatenate([jnp.ones_like(running[:, :1]), running[:, :-1]], axis=1)
    rendered = jnp.sum(prefix[:, :, None, :] * colour, axis=1)

    def compose(earlier, later):
        return (earlier[0] * later[0], later[1] + later[0][:, :, None, :] * earlier[1])

    flipped = lax.associative_scan(compose, (transmit[:, ::-1], colour[:, ::-1]), axis=1)
    suffix = flipped[1][:, ::-1]
    behind = jnp.concatenate([suffix[:, 1:], jnp.zeros_like(suffix[:, :1])], axis=1)
    upstream_cot = jnp.transpose(cotangent, (1, 0, 2))
    grad_colour = prefix[:, :, None, :] * upstream_cot[:, None]
    grad_transmit = prefix * jnp.sum(upstream_cot[:, None] * behind, axis=2)
    grad_ordered = jnp.concatenate([grad_colour, grad_transmit[:, :, None, :]], axis=2)
    upstream = jnp.einsum(
        "irk,ircp->kicp", ranks_onehot, grad_ordered, precision=lax.Precision.HIGHEST
    )
    return (jnp.transpose(rendered, (1, 0, 2)), upstream)


def local(geometry, opacity, colours, coverage, gauss_lists, orders, cotangent):
    parts_count = lax.axis_size("dom")
    group_index = lax.axis_index("tile")
    tiles_per = orders.shape[0]
    pixels = cotangent.shape[2]
    params = jnp.concatenate([geometry, opacity[None, :], colours], axis=0)
    gauss_total = params.shape[1]
    tile_ids = coverage[0, 0]
    entries = gauss_lists[0, 0]
    slots_count = tile_ids.shape[0]
    turn_rows = math.gcd(slots_count, 4)
    covered = jnp.sum((tile_ids >= 0).astype(jnp.int32))
    turn_count = (covered + turn_rows - 1) // turn_rows
    pixel_x, pixel_y = pixel_grid(tile_ids, group_index, tiles_per, pixels)
    default = jnp.concatenate(
        [jnp.zeros((3, pixels), jnp.float32), jnp.ones((1, pixels), jnp.float32)], axis=0
    )

    live_all = entries >= 0
    chosen_all = jnp.take(params, jnp.where(live_all, entries, 0), axis=1)
    live_all_f = live_all.astype(jnp.float32)

    def gather_turn(first_row):
        index_rows = lax.dynamic_slice_in_dim(entries, first_row, turn_rows, 0)
        live = lax.dynamic_slice_in_dim(live_all_f, first_row, turn_rows, 0)
        chosen = lax.dynamic_slice_in_dim(chosen_all, first_row, turn_rows, 1)
        rows_x = lax.dynamic_slice_in_dim(pixel_x, first_row, turn_rows, 0)
        rows_y = lax.dynamic_slice_in_dim(pixel_y, first_row, turn_rows, 0)
        return (index_rows, live, chosen, rows_x, rows_y)

    def forward_turn(turn_index, partial_value):
        first_row = turn_index * turn_rows
        index_rows, live_mask, chosen, rows_x, rows_y = gather_turn(first_row)
        colour, transmit = render(chosen, rows_x, rows_y, live_mask)
        packed = jnp.concatenate([colour, transmit[:, None, :]], axis=1)
        return lax.dynamic_update_slice_in_dim(partial_value, packed, first_row, 0)

    partial_value = lax.fori_loop(
        0, turn_count, forward_turn, jnp.broadcast_to(default, (slots_count, 4, pixels))
    )
    block_slots = parts_count * tiles_per
    target = jnp.where(tile_ids >= 0, tile_ids, block_slots)
    dense = (
        jnp.broadcast_to(default, (block_slots, 4, pixels))
        .at[target]
        .set(partial_value, mode="drop")
    )
    arrived = lax.all_to_all(
        dense.reshape(parts_count, tiles_per, 4, pixels),
        "dom",
        split_axis=0,
        concat_axis=0,
        tiled=True,
    )
    rendered, upstream = composite(arrived, orders, cotangent)
    returned = lax.all_to_all(upstream, "dom", split_axis=0, concat_axis=0, tiled=True)
    slot_grads = jnp.take(
        returned.reshape(block_slots, 4, pixels), jnp.maximum(tile_ids, 0), axis=0
    )

    def backward_turn(turn_index, compact):
        first_row = turn_index * turn_rows
        index_rows, live_mask, chosen, rows_x, rows_y = gather_turn(first_row)
        upper_cot = lax.dynamic_slice_in_dim(slot_grads, first_row, turn_rows, 0)
        _, pullback = jax.vjp(lambda values: render(values, rows_x, rows_y, live_mask), chosen)
        grad_chosen = pullback((upper_cot[:, :3], upper_cot[:, 3]))[0]
        return lax.dynamic_update_slice_in_dim(compact, grad_chosen, first_row, 1)

    compact = lax.fori_loop(
        0, turn_count, backward_turn, jnp.zeros(chosen_all.shape, jnp.float32)
    )
    rows_count = params.shape[0]
    groups_count = lax.axis_size("tile")
    shard = gauss_total // groups_count
    lo_size = 48 if shard % 48 == 0 else 1
    hi_size = gauss_total // lo_size
    values = jnp.where(live_all[None], compact, 0.0)
    values = jnp.transpose(values, (1, 2, 0)).reshape(-1, rows_count)
    flat_index = jnp.where(live_all, entries, -1).reshape(-1)
    hi_index = jnp.where(flat_index >= 0, flat_index // lo_size, -1)
    lo_index = flat_index % lo_size
    hi_hot = (hi_index[:, None] == jnp.arange(hi_size, dtype=jnp.int32)[None, :]).astype(
        jnp.float32
    )
    lo_hot = (lo_index[:, None] == jnp.arange(lo_size, dtype=jnp.int32)[None, :]).astype(
        jnp.float32
    )
    spread = (lo_hot[:, :, None] * values[:, None, :]).reshape(-1, lo_size * rows_count)
    placed = jnp.einsum("eh,ez->hz", hi_hot, spread, precision=lax.Precision.HIGHEST)
    blocks = placed.reshape(groups_count, hi_size // groups_count, lo_size * rows_count)
    total = lax.dynamic_index_in_dim(blocks, group_index, 0, keepdims=False)
    for step in range(1, groups_count):
        outgoing = lax.dynamic_index_in_dim(
            blocks, (group_index + step) % groups_count, 0, keepdims=False
        )
        total = total + lax.ppermute(
            outgoing,
            "tile",
            perm=[(i, (i + step) % groups_count) for i in range(groups_count)],
        )
    shares = jnp.transpose(
        total.reshape(hi_size // groups_count, lo_size, rows_count), (2, 0, 1)
    ).reshape(rows_count, shard)
    return (rendered, shares[:5], shares[5], shares[6:])


def solution(mesh):
    placed = (
        P(None, "dom"),
        P("dom"),
        P(None, "dom"),
        P("dom", "tile", None),
        P("dom", "tile", None, None),
        P(("dom", "tile"), None),
        P(None, ("dom", "tile"), None),
    )
    return jax.shard_map(
        local,
        mesh=mesh,
        in_specs=placed,
        out_specs=(
            P(None, ("dom", "tile"), None),
            P(None, ("dom", "tile")),
            P(("dom", "tile")),
            P(None, ("dom", "tile")),
        ),
        check_vma=False,
    )
```

```python
import math

import jax
import jax.numpy as jnp
from jax import lax
from jax.sharding import PartitionSpec as P

TSIDE = 16


def render(params, pixel_x, pixel_y, live_mask):
    centre_x = params[0][:, None, :]
    centre_y = params[1][:, None, :]
    inv_one = jnp.exp(-2.0 * params[2])
    inv_two = jnp.exp(-2.0 * params[3])
    cosine = jnp.cos(params[4])
    sine_angle = jnp.sin(params[4])
    coef_a = (cosine * cosine * inv_one + sine_angle * sine_angle * inv_two)[:, None, :]
    coef_b = (cosine * sine_angle * (inv_one - inv_two))[:, None, :]
    coef_c = (sine_angle * sine_angle * inv_one + cosine * cosine * inv_two)[:, None, :]
    delta_x = pixel_x[:, :, None] - centre_x
    delta_y = pixel_y[:, :, None] - centre_y
    quadratic = (
        coef_a * delta_x * delta_x + 2.0 * coef_b * delta_x * delta_y + coef_c * delta_y * delta_y
    )
    strength = jax.nn.sigmoid(params[5]) * live_mask
    opaque_part = strength[:, None, :] * jnp.exp(-0.5 * quadratic)
    log_keep = jnp.log1p(-opaque_part)
    entries_count = log_keep.shape[2]
    ahead = (
        jnp.arange(entries_count, dtype=jnp.int32)[:, None]
        < jnp.arange(entries_count, dtype=jnp.int32)[None, :]
    ).astype(jnp.float32)
    before = jnp.einsum("kpg,gh->kph", log_keep, ahead, precision=lax.Precision.HIGHEST)
    weight = opaque_part * jnp.exp(before)
    colour = jnp.einsum("kpg,ckg->kcp", weight, params[6:9], precision=lax.Precision.HIGHEST)
    transmit = jnp.exp(jnp.sum(log_keep, axis=2))
    return (colour, transmit)


def pixel_grid(tile_ids, group_index, tiles_per, pixels):
    safe_ids = jnp.maximum(tile_ids, 0)
    block_row = safe_ids // tiles_per
    column = group_index * tiles_per + safe_ids % tiles_per
    within = jnp.arange(pixels, dtype=jnp.int32)
    pixel_x = (column[:, None] * TSIDE + within[None, :] % TSIDE).astype(jnp.float32) + 0.5
    pixel_y = (block_row[:, None] * TSIDE + within[None, :] // TSIDE).astype(jnp.float32) + 0.5
    return (pixel_x, pixel_y)


def composite(arrived, orders, cotangent):
    parts_count = arrived.shape[0]
    ranks_onehot = (
        orders[:, None, :] == jnp.arange(parts_count, dtype=jnp.int32)[None, :, None]
    ).astype(jnp.float32)
    ordered = jnp.einsum("irk,kicp->ircp", ranks_onehot, arrived, precision=lax.Precision.HIGHEST)
    colour = ordered[:, :, :3]
    transmit = ordered[:, :, 3]
    running = jnp.cumprod(transmit, axis=1)
    prefix = jnp.concatenate([jnp.ones_like(running[:, :1]), running[:, :-1]], axis=1)
    rendered = jnp.sum(prefix[:, :, None, :] * colour, axis=1)

    def compose(earlier, later):
        return (earlier[0] * later[0], later[1] + later[0][:, :, None, :] * earlier[1])

    flipped = lax.associative_scan(compose, (transmit[:, ::-1], colour[:, ::-1]), axis=1)
    suffix = flipped[1][:, ::-1]
    behind = jnp.concatenate([suffix[:, 1:], jnp.zeros_like(suffix[:, :1])], axis=1)
    upstream_cot = jnp.transpose(cotangent, (1, 0, 2))
    grad_colour = prefix[:, :, None, :] * upstream_cot[:, None]
    grad_transmit = prefix * jnp.sum(upstream_cot[:, None] * behind, axis=2)
    grad_ordered = jnp.concatenate([grad_colour, grad_transmit[:, :, None, :]], axis=2)
    upstream = jnp.einsum(
        "irk,ircp->kicp", ranks_onehot, grad_ordered, precision=lax.Precision.HIGHEST
    )
    return (jnp.transpose(rendered, (1, 0, 2)), upstream)


def local(geometry, opacity, colours, coverage, gauss_lists, orders, cotangent):
    parts_count = lax.axis_size("dom")
    group_index = lax.axis_index("tile")
    tiles_per = orders.shape[0]
    pixels = cotangent.shape[2]
    params = jnp.concatenate([geometry, opacity[None, :], colours], axis=0)
    gauss_total = params.shape[1]
    tile_ids = coverage[0, 0]
    entries = gauss_lists[0, 0]
    slots_count = tile_ids.shape[0]
    turn_rows = math.gcd(slots_count, 4)
    covered = jnp.sum((tile_ids >= 0).astype(jnp.int32))
    turn_count = (covered + turn_rows - 1) // turn_rows
    pixel_x, pixel_y = pixel_grid(tile_ids, group_index, tiles_per, pixels)
    default = jnp.concatenate(
        [jnp.zeros((3, pixels), jnp.float32), jnp.ones((1, pixels), jnp.float32)], axis=0
    )

    live_all = entries >= 0
    chosen_all = jnp.take(params, jnp.where(live_all, entries, 0), axis=1)
    live_all_f = live_all.astype(jnp.float32)

    def gather_turn(first_row):
        index_rows = lax.dynamic_slice_in_dim(entries, first_row, turn_rows, 0)
        live = lax.dynamic_slice_in_dim(live_all_f, first_row, turn_rows, 0)
        chosen = lax.dynamic_slice_in_dim(chosen_all, first_row, turn_rows, 1)
        rows_x = lax.dynamic_slice_in_dim(pixel_x, first_row, turn_rows, 0)
        rows_y = lax.dynamic_slice_in_dim(pixel_y, first_row, turn_rows, 0)
        return (index_rows, live, chosen, rows_x, rows_y)

    def forward_turn(turn_index, partial_value):
        first_row = turn_index * turn_rows
        index_rows, live_mask, chosen, rows_x, rows_y = gather_turn(first_row)
        colour, transmit = render(chosen, rows_x, rows_y, live_mask)
        packed = jnp.concatenate([colour, transmit[:, None, :]], axis=1)
        return lax.dynamic_update_slice_in_dim(partial_value, packed, first_row, 0)

    partial_value = lax.fori_loop(
        0, turn_count, forward_turn, jnp.broadcast_to(default, (slots_count, 4, pixels))
    )
    block_slots = parts_count * tiles_per
    target = jnp.where(tile_ids >= 0, tile_ids, block_slots)
    dense = (
        jnp.broadcast_to(default, (block_slots, 4, pixels))
        .at[target]
        .set(partial_value, mode="drop")
    )
    arrived = lax.all_to_all(
        dense.reshape(parts_count, tiles_per, 4, pixels),
        "dom",
        split_axis=0,
        concat_axis=0,
        tiled=True,
    )
    rendered, upstream = composite(arrived, orders, cotangent)
    returned = lax.all_to_all(upstream, "dom", split_axis=0, concat_axis=0, tiled=True)
    slot_grads = jnp.take(
        returned.reshape(block_slots, 4, pixels), jnp.maximum(tile_ids, 0), axis=0
    )

    def backward_turn(turn_index, compact):
        first_row = turn_index * turn_rows
        index_rows, live_mask, chosen, rows_x, rows_y = gather_turn(first_row)
        upper_cot = lax.dynamic_slice_in_dim(slot_grads, first_row, turn_rows, 0)
        _, pullback = jax.vjp(lambda values: render(values, rows_x, rows_y, live_mask), chosen)
        grad_chosen = pullback((upper_cot[:, :3], upper_cot[:, 3]))[0]
        return lax.dynamic_update_slice_in_dim(compact, grad_chosen, first_row, 1)

    compact = lax.fori_loop(
        0, turn_count, backward_turn, jnp.zeros(chosen_all.shape, jnp.float32)
    )
    rows_count = params.shape[0]
    groups_count = lax.axis_size("tile")
    shard = gauss_total // groups_count
    lo_size = 48 if shard % 48 == 0 else 1
    hi_size = gauss_total // lo_size
    values = jnp.where(live_all[None], compact, 0.0)
    values = jnp.transpose(values, (1, 2, 0)).reshape(-1, rows_count)
    flat_index = jnp.where(live_all, entries, -1).reshape(-1)
    hi_index = jnp.where(flat_index >= 0, flat_index // lo_size, -1)
    lo_index = flat_index % lo_size
    hi_hot = (hi_index[:, None] == jnp.arange(hi_size, dtype=jnp.int32)[None, :]).astype(
        jnp.float32
    )
    lo_hot = (lo_index[:, None] == jnp.arange(lo_size, dtype=jnp.int32)[None, :]).astype(
        jnp.float32
    )
    spread = (lo_hot[:, :, None] * values[:, None, :]).reshape(-1, lo_size * rows_count)
    placed = jnp.einsum("eh,ez->hz", hi_hot, spread, precision=lax.Precision.HIGHEST)
    blocks = placed.reshape(groups_count, hi_size // groups_count, lo_size * rows_count)
    total = lax.dynamic_index_in_dim(blocks, group_index, 0, keepdims=False)
    for step in range(1, groups_count):
        outgoing = lax.dynamic_index_in_dim(
            blocks, (group_index + step) % groups_count, 0, keepdims=False
        )
        total = total + lax.ppermute(
            outgoing,
            "tile",
            perm=[(i, (i + step) % groups_count) for i in range(groups_count)],
        )
    shares = jnp.transpose(
        total.reshape(hi_size // groups_count, lo_size, rows_count), (2, 0, 1)
    ).reshape(rows_count, shard)
    return (rendered, shares[:5], shares[5], shares[6:])


def solution(mesh):
    placed = (
        P(None, "dom"),
        P("dom"),
        P(None, "dom"),
        P("dom", "tile", None),
        P("dom", "tile", None, None),
        P(("dom", "tile"), None),
        P(None, ("dom", "tile"), None),
    )
    return jax.shard_map(
        local,
        mesh=mesh,
        in_specs=placed,
        out_specs=(
            P(None, ("dom", "tile"), None),
            P(None, ("dom", "tile")),
            P(("dom", "tile")),
            P(None, ("dom", "tile")),
        ),
        check_vma=False,
    )
```

```python
import math

import jax
import jax.numpy as jnp
from jax import lax
from jax.sharding import PartitionSpec as P

TSIDE = 16


def render(params, pixel_x, pixel_y, live_mask):
    centre_x = params[0][:, None, :]
    centre_y = params[1][:, None, :]
    inv_one = jnp.exp(-2.0 * params[2])
    inv_two = jnp.exp(-2.0 * params[3])
    cosine = jnp.cos(params[4])
    sine_angle = jnp.sin(params[4])
    coef_a = (cosine * cosine * inv_one + sine_angle * sine_angle * inv_two)[:, None, :]
    coef_b = (cosine * sine_angle * (inv_one - inv_two))[:, None, :]
    coef_c = (sine_angle * sine_angle * inv_one + cosine * cosine * inv_two)[:, None, :]
    delta_x = pixel_x[:, :, None] - centre_x
    delta_y = pixel_y[:, :, None] - centre_y
    quadratic = (
        coef_a * delta_x * delta_x + 2.0 * coef_b * delta_x * delta_y + coef_c * delta_y * delta_y
    )
    strength = jax.nn.sigmoid(params[5]) * live_mask
    opaque_part = strength[:, None, :] * jnp.exp(-0.5 * quadratic)
    log_keep = jnp.log1p(-opaque_part)
    entries_count = log_keep.shape[2]
    ahead = (
        jnp.arange(entries_count, dtype=jnp.int32)[:, None]
        < jnp.arange(entries_count, dtype=jnp.int32)[None, :]
    ).astype(jnp.float32)
    before = jnp.einsum("kpg,gh->kph", log_keep, ahead, precision=lax.Precision.HIGHEST)
    weight = opaque_part * jnp.exp(before)
    colour = jnp.einsum("kpg,ckg->kcp", weight, params[6:9], precision=lax.Precision.HIGHEST)
    transmit = jnp.exp(jnp.sum(log_keep, axis=2))
    return (colour, transmit)


def pixel_grid(tile_ids, group_index, tiles_per, pixels):
    safe_ids = jnp.maximum(tile_ids, 0)
    block_row = safe_ids // tiles_per
    column = group_index * tiles_per + safe_ids % tiles_per
    within = jnp.arange(pixels, dtype=jnp.int32)
    pixel_x = (column[:, None] * TSIDE + within[None, :] % TSIDE).astype(jnp.float32) + 0.5
    pixel_y = (block_row[:, None] * TSIDE + within[None, :] // TSIDE).astype(jnp.float32) + 0.5
    return (pixel_x, pixel_y)


def composite(arrived, orders, cotangent):
    parts_count = arrived.shape[0]
    ranks_onehot = (
        orders[:, None, :] == jnp.arange(parts_count, dtype=jnp.int32)[None, :, None]
    ).astype(jnp.float32)
    ordered = jnp.einsum("irk,kicp->ircp", ranks_onehot, arrived, precision=lax.Precision.HIGHEST)
    colour = ordered[:, :, :3]
    transmit = ordered[:, :, 3]
    running = jnp.cumprod(transmit, axis=1)
    prefix = jnp.concatenate([jnp.ones_like(running[:, :1]), running[:, :-1]], axis=1)
    rendered = jnp.sum(prefix[:, :, None, :] * colour, axis=1)

    def compose(earlier, later):
        return (earlier[0] * later[0], later[1] + later[0][:, :, None, :] * earlier[1])

    flipped = lax.associative_scan(compose, (transmit[:, ::-1], colour[:, ::-1]), axis=1)
    suffix = flipped[1][:, ::-1]
    behind = jnp.concatenate([suffix[:, 1:], jnp.zeros_like(suffix[:, :1])], axis=1)
    upstream_cot = jnp.transpose(cotangent, (1, 0, 2))
    grad_colour = prefix[:, :, None, :] * upstream_cot[:, None]
    grad_transmit = prefix * jnp.sum(upstream_cot[:, None] * behind, axis=2)
    grad_ordered = jnp.concatenate([grad_colour, grad_transmit[:, :, None, :]], axis=2)
    upstream = jnp.einsum(
        "irk,ircp->kicp", ranks_onehot, grad_ordered, precision=lax.Precision.HIGHEST
    )
    return (jnp.transpose(rendered, (1, 0, 2)), upstream)


def local(geometry, opacity, colours, coverage, gauss_lists, orders, cotangent):
    parts_count = lax.axis_size("dom")
    group_index = lax.axis_index("tile")
    tiles_per = orders.shape[0]
    pixels = cotangent.shape[2]
    params = jnp.concatenate([geometry, opacity[None, :], colours], axis=0)
    gauss_total = params.shape[1]
    tile_ids = coverage[0, 0]
    entries = gauss_lists[0, 0]
    slots_count = tile_ids.shape[0]
    turn_rows = math.gcd(slots_count, 4)
    covered = jnp.sum((tile_ids >= 0).astype(jnp.int32))
    turn_count = (covered + turn_rows - 1) // turn_rows
    pixel_x, pixel_y = pixel_grid(tile_ids, group_index, tiles_per, pixels)
    default = jnp.concatenate(
        [jnp.zeros((3, pixels), jnp.float32), jnp.ones((1, pixels), jnp.float32)], axis=0
    )

    live_all = entries >= 0
    chosen_all = jnp.take(params, jnp.where(live_all, entries, 0), axis=1)
    live_all_f = live_all.astype(jnp.float32)

    def gather_turn(first_row):
        index_rows = lax.dynamic_slice_in_dim(entries, first_row, turn_rows, 0)
        live = lax.dynamic_slice_in_dim(live_all_f, first_row, turn_rows, 0)
        chosen = lax.dynamic_slice_in_dim(chosen_all, first_row, turn_rows, 1)
        rows_x = lax.dynamic_slice_in_dim(pixel_x, first_row, turn_rows, 0)
        rows_y = lax.dynamic_slice_in_dim(pixel_y, first_row, turn_rows, 0)
        return (index_rows, live, chosen, rows_x, rows_y)

    def forward_turn(turn_index, partial_value):
        first_row = turn_index * turn_rows
        index_rows, live_mask, chosen, rows_x, rows_y = gather_turn(first_row)
        colour, transmit = render(chosen, rows_x, rows_y, live_mask)
        packed = jnp.concatenate([colour, transmit[:, None, :]], axis=1)
        return lax.dynamic_update_slice_in_dim(partial_value, packed, first_row, 0)

    partial_value = lax.fori_loop(
        0, turn_count, forward_turn, jnp.broadcast_to(default, (slots_count, 4, pixels))
    )
    block_slots = parts_count * tiles_per
    target = jnp.where(tile_ids >= 0, tile_ids, block_slots)
    dense = (
        jnp.broadcast_to(default, (block_slots, 4, pixels))
        .at[target]
        .set(partial_value, mode="drop")
    )
    arrived = lax.all_to_all(
        dense.reshape(parts_count, tiles_per, 4, pixels),
        "dom",
        split_axis=0,
        concat_axis=0,
        tiled=True,
    )
    rendered, upstream = composite(arrived, orders, cotangent)
    returned = lax.all_to_all(upstream, "dom", split_axis=0, concat_axis=0, tiled=True)
    slot_grads = jnp.take(
        returned.reshape(block_slots, 4, pixels), jnp.maximum(tile_ids, 0), axis=0
    )

    def backward_turn(turn_index, compact):
        first_row = turn_index * turn_rows
        index_rows, live_mask, chosen, rows_x, rows_y = gather_turn(first_row)
        upper_cot = lax.dynamic_slice_in_dim(slot_grads, first_row, turn_rows, 0)
        _, pullback = jax.vjp(lambda values: render(values, rows_x, rows_y, live_mask), chosen)
        grad_chosen = pullback((upper_cot[:, :3], upper_cot[:, 3]))[0]
        return lax.dynamic_update_slice_in_dim(compact, grad_chosen, first_row, 1)

    compact = lax.fori_loop(
        0, turn_count, backward_turn, jnp.zeros(chosen_all.shape, jnp.float32)
    )
    rows_count = params.shape[0]
    groups_count = lax.axis_size("tile")
    shard = gauss_total // groups_count
    lo_size = 384 if shard % 384 == 0 else shard
    hi_size = gauss_total // lo_size
    flat_index = jnp.where(live_all, entries, -1).reshape(-1)
    values = jnp.where(live_all[None], compact, 0.0).reshape(rows_count, -1)
    hi_index = jnp.where(flat_index >= 0, flat_index // lo_size, -1)
    lo_index = flat_index % lo_size
    spread = values[:, None, :] * (
        hi_index[None, None, :] == jnp.arange(hi_size, dtype=jnp.int32)[None, :, None]
    ).astype(jnp.float32)
    lo_hot = (lo_index[None, :] == jnp.arange(lo_size, dtype=jnp.int32)[:, None]).astype(
        jnp.float32
    )
    placed = jnp.einsum("che,le->chl", spread, lo_hot, precision=lax.Precision.HIGHEST)
    gathered = lax.all_to_all(placed, "tile", split_axis=1, concat_axis=1, tiled=True)
    total = jnp.sum(
        gathered.reshape(rows_count, groups_count, hi_size // groups_count, lo_size), axis=1
    )
    shares = total.reshape(rows_count, shard)
    return (rendered, shares[:5], shares[5], shares[6:])


def solution(mesh):
    placed = (
        P(None, "dom"),
        P("dom"),
        P(None, "dom"),
        P("dom", "tile", None),
        P("dom", "tile", None, None),
        P(("dom", "tile"), None),
        P(None, ("dom", "tile"), None),
    )
    return jax.shard_map(
        local,
        mesh=mesh,
        in_specs=placed,
        out_specs=(
            P(None, ("dom", "tile"), None),
            P(None, ("dom", "tile")),
            P(("dom", "tile")),
            P(None, ("dom", "tile")),
        ),
        check_vma=False,
    )
```

```python
import math

import jax
import jax.numpy as jnp
from jax import lax
from jax.sharding import PartitionSpec as P

TSIDE = 16


def render(params, pixel_x, pixel_y, live_mask):
    centre_x = params[0][:, None, :]
    centre_y = params[1][:, None, :]
    inv_one = jnp.exp(-2.0 * params[2])
    inv_two = jnp.exp(-2.0 * params[3])
    cosine = jnp.cos(params[4])
    sine_angle = jnp.sin(params[4])
    coef_a = (cosine * cosine * inv_one + sine_angle * sine_angle * inv_two)[:, None, :]
    coef_b = (cosine * sine_angle * (inv_one - inv_two))[:, None, :]
    coef_c = (sine_angle * sine_angle * inv_one + cosine * cosine * inv_two)[:, None, :]
    delta_x = pixel_x[:, :, None] - centre_x
    delta_y = pixel_y[:, :, None] - centre_y
    quadratic = (
        coef_a * delta_x * delta_x + 2.0 * coef_b * delta_x * delta_y + coef_c * delta_y * delta_y
    )
    strength = jax.nn.sigmoid(params[5]) * live_mask
    opaque_part = strength[:, None, :] * jnp.exp(-0.5 * quadratic)
    log_keep = jnp.log1p(-opaque_part)
    entries_count = log_keep.shape[2]
    ahead = (
        jnp.arange(entries_count, dtype=jnp.int32)[:, None]
        < jnp.arange(entries_count, dtype=jnp.int32)[None, :]
    ).astype(jnp.float32)
    before = jnp.einsum("kpg,gh->kph", log_keep, ahead, precision=lax.Precision.HIGHEST)
    weight = opaque_part * jnp.exp(before)
    colour = jnp.einsum("kpg,ckg->kcp", weight, params[6:9], precision=lax.Precision.HIGHEST)
    transmit = jnp.exp(jnp.sum(log_keep, axis=2))
    return (colour, transmit)


def pixel_grid(tile_ids, group_index, tiles_per, pixels):
    safe_ids = jnp.maximum(tile_ids, 0)
    block_row = safe_ids // tiles_per
    column = group_index * tiles_per + safe_ids % tiles_per
    within = jnp.arange(pixels, dtype=jnp.int32)
    pixel_x = (column[:, None] * TSIDE + within[None, :] % TSIDE).astype(jnp.float32) + 0.5
    pixel_y = (block_row[:, None] * TSIDE + within[None, :] // TSIDE).astype(jnp.float32) + 0.5
    return (pixel_x, pixel_y)


def composite(arrived, orders, cotangent):
    parts_count = arrived.shape[0]
    ranks_onehot = (
        orders[:, None, :] == jnp.arange(parts_count, dtype=jnp.int32)[None, :, None]
    ).astype(jnp.float32)
    ordered = jnp.einsum("irk,kicp->ircp", ranks_onehot, arrived, precision=lax.Precision.HIGHEST)
    colour = ordered[:, :, :3]
    transmit = ordered[:, :, 3]
    running = jnp.cumprod(transmit, axis=1)
    prefix = jnp.concatenate([jnp.ones_like(running[:, :1]), running[:, :-1]], axis=1)
    rendered = jnp.sum(prefix[:, :, None, :] * colour, axis=1)

    def compose(earlier, later):
        return (earlier[0] * later[0], later[1] + later[0][:, :, None, :] * earlier[1])

    flipped = lax.associative_scan(compose, (transmit[:, ::-1], colour[:, ::-1]), axis=1)
    suffix = flipped[1][:, ::-1]
    behind = jnp.concatenate([suffix[:, 1:], jnp.zeros_like(suffix[:, :1])], axis=1)
    upstream_cot = jnp.transpose(cotangent, (1, 0, 2))
    grad_colour = prefix[:, :, None, :] * upstream_cot[:, None]
    grad_transmit = prefix * jnp.sum(upstream_cot[:, None] * behind, axis=2)
    grad_ordered = jnp.concatenate([grad_colour, grad_transmit[:, :, None, :]], axis=2)
    upstream = jnp.einsum(
        "irk,ircp->kicp", ranks_onehot, grad_ordered, precision=lax.Precision.HIGHEST
    )
    return (jnp.transpose(rendered, (1, 0, 2)), upstream)


def local(geometry, opacity, colours, coverage, gauss_lists, orders, cotangent):
    parts_count = lax.axis_size("dom")
    group_index = lax.axis_index("tile")
    tiles_per = orders.shape[0]
    pixels = cotangent.shape[2]
    params = jnp.concatenate([geometry, opacity[None, :], colours], axis=0)
    gauss_total = params.shape[1]
    tile_ids = coverage[0, 0]
    entries = gauss_lists[0, 0]
    slots_count = tile_ids.shape[0]
    turn_rows = math.gcd(slots_count, 4)
    covered = jnp.sum((tile_ids >= 0).astype(jnp.int32))
    turn_count = (covered + turn_rows - 1) // turn_rows
    pixel_x, pixel_y = pixel_grid(tile_ids, group_index, tiles_per, pixels)
    default = jnp.concatenate(
        [jnp.zeros((3, pixels), jnp.float32), jnp.ones((1, pixels), jnp.float32)], axis=0
    )

    live_all = entries >= 0
    groups_count = lax.axis_size("tile")
    shard = gauss_total // groups_count
    lo_size = 384 if shard % 384 == 0 else shard
    hi_size = gauss_total // lo_size
    safe_index = jnp.where(live_all, entries, 0).reshape(-1)
    hi_pick = (
        safe_index[None, None, :] // lo_size
        == jnp.arange(hi_size, dtype=jnp.int32)[None, :, None]
    ).astype(jnp.float32)
    lo_pick = (
        safe_index[None, :] % lo_size == jnp.arange(lo_size, dtype=jnp.int32)[:, None]
    ).astype(jnp.float32)
    by_row = jnp.einsum(
        "chl,le->che",
        params.reshape(params.shape[0], hi_size, lo_size),
        lo_pick,
        precision=lax.Precision.HIGHEST,
    )
    chosen_all = jnp.sum(by_row * hi_pick, axis=1).reshape((params.shape[0],) + entries.shape)
    live_all_f = live_all.astype(jnp.float32)

    def gather_turn(first_row):
        index_rows = lax.dynamic_slice_in_dim(entries, first_row, turn_rows, 0)
        live = lax.dynamic_slice_in_dim(live_all_f, first_row, turn_rows, 0)
        chosen = lax.dynamic_slice_in_dim(chosen_all, first_row, turn_rows, 1)
        rows_x = lax.dynamic_slice_in_dim(pixel_x, first_row, turn_rows, 0)
        rows_y = lax.dynamic_slice_in_dim(pixel_y, first_row, turn_rows, 0)
        return (index_rows, live, chosen, rows_x, rows_y)

    def forward_turn(turn_index, partial_value):
        first_row = turn_index * turn_rows
        index_rows, live_mask, chosen, rows_x, rows_y = gather_turn(first_row)
        colour, transmit = render(chosen, rows_x, rows_y, live_mask)
        packed = jnp.concatenate([colour, transmit[:, None, :]], axis=1)
        return lax.dynamic_update_slice_in_dim(partial_value, packed, first_row, 0)

    partial_value = lax.fori_loop(
        0, turn_count, forward_turn, jnp.broadcast_to(default, (slots_count, 4, pixels))
    )
    block_slots = parts_count * tiles_per
    target = jnp.where(tile_ids >= 0, tile_ids, block_slots)
    dense = (
        jnp.broadcast_to(default, (block_slots, 4, pixels))
        .at[target]
        .set(partial_value, mode="drop")
    )
    arrived = lax.all_to_all(
        dense.reshape(parts_count, tiles_per, 4, pixels),
        "dom",
        split_axis=0,
        concat_axis=0,
        tiled=True,
    )
    rendered, upstream = composite(arrived, orders, cotangent)
    returned = lax.all_to_all(upstream, "dom", split_axis=0, concat_axis=0, tiled=True)
    slot_grads = jnp.take(
        returned.reshape(block_slots, 4, pixels), jnp.maximum(tile_ids, 0), axis=0
    )

    def backward_turn(turn_index, compact):
        first_row = turn_index * turn_rows
        index_rows, live_mask, chosen, rows_x, rows_y = gather_turn(first_row)
        upper_cot = lax.dynamic_slice_in_dim(slot_grads, first_row, turn_rows, 0)
        _, pullback = jax.vjp(lambda values: render(values, rows_x, rows_y, live_mask), chosen)
        grad_chosen = pullback((upper_cot[:, :3], upper_cot[:, 3]))[0]
        return lax.dynamic_update_slice_in_dim(compact, grad_chosen, first_row, 1)

    compact = lax.fori_loop(
        0, turn_count, backward_turn, jnp.zeros(chosen_all.shape, jnp.float32)
    )
    rows_count = params.shape[0]
    flat_index = jnp.where(live_all, entries, -1).reshape(-1)
    values = jnp.where(live_all[None], compact, 0.0).reshape(rows_count, -1)
    hi_index = jnp.where(flat_index >= 0, flat_index // lo_size, -1)
    lo_index = flat_index % lo_size
    spread = values[:, None, :] * (
        hi_index[None, None, :] == jnp.arange(hi_size, dtype=jnp.int32)[None, :, None]
    ).astype(jnp.float32)
    lo_hot = (lo_index[None, :] == jnp.arange(lo_size, dtype=jnp.int32)[:, None]).astype(
        jnp.float32
    )
    placed = jnp.einsum("che,le->chl", spread, lo_hot, precision=lax.Precision.HIGHEST)
    gathered = lax.all_to_all(placed, "tile", split_axis=1, concat_axis=1, tiled=True)
    total = jnp.sum(
        gathered.reshape(rows_count, groups_count, hi_size // groups_count, lo_size), axis=1
    )
    shares = total.reshape(rows_count, shard)
    return (rendered, shares[:5], shares[5], shares[6:])


def solution(mesh):
    placed = (
        P(None, "dom"),
        P("dom"),
        P(None, "dom"),
        P("dom", "tile", None),
        P("dom", "tile", None, None),
        P(("dom", "tile"), None),
        P(None, ("dom", "tile"), None),
    )
    return jax.shard_map(
        local,
        mesh=mesh,
        in_specs=placed,
        out_specs=(
            P(None, ("dom", "tile"), None),
            P(None, ("dom", "tile")),
            P(("dom", "tile")),
            P(None, ("dom", "tile")),
        ),
        check_vma=False,
    )
```

```python
import math

import jax
import jax.numpy as jnp
from jax import lax
from jax.sharding import PartitionSpec as P

TSIDE = 16


def render(params, pixel_x, pixel_y, live_mask):
    centre_x = params[0][:, None, :]
    centre_y = params[1][:, None, :]
    inv_one = jnp.exp(-2.0 * params[2])
    inv_two = jnp.exp(-2.0 * params[3])
    cosine = jnp.cos(params[4])
    sine_angle = jnp.sin(params[4])
    coef_a = (cosine * cosine * inv_one + sine_angle * sine_angle * inv_two)[:, None, :]
    coef_b = (cosine * sine_angle * (inv_one - inv_two))[:, None, :]
    coef_c = (sine_angle * sine_angle * inv_one + cosine * cosine * inv_two)[:, None, :]
    delta_x = pixel_x[:, :, None] - centre_x
    delta_y = pixel_y[:, :, None] - centre_y
    quadratic = (
        coef_a * delta_x * delta_x + 2.0 * coef_b * delta_x * delta_y + coef_c * delta_y * delta_y
    )
    strength = jax.nn.sigmoid(params[5]) * live_mask
    opaque_part = strength[:, None, :] * jnp.exp(-0.5 * quadratic)
    log_keep = jnp.log1p(-opaque_part)
    entries_count = log_keep.shape[2]
    ahead = (
        jnp.arange(entries_count, dtype=jnp.int32)[:, None]
        < jnp.arange(entries_count, dtype=jnp.int32)[None, :]
    ).astype(jnp.float32)
    before = jnp.einsum("kpg,gh->kph", log_keep, ahead, precision=lax.Precision.HIGHEST)
    weight = opaque_part * jnp.exp(before)
    colour = jnp.einsum("kpg,ckg->kcp", weight, params[6:9], precision=lax.Precision.HIGHEST)
    transmit = jnp.exp(jnp.sum(log_keep, axis=2))
    return (colour, transmit)


def pixel_grid(tile_ids, group_index, tiles_per, pixels):
    safe_ids = jnp.maximum(tile_ids, 0)
    block_row = safe_ids // tiles_per
    column = group_index * tiles_per + safe_ids % tiles_per
    within = jnp.arange(pixels, dtype=jnp.int32)
    pixel_x = (column[:, None] * TSIDE + within[None, :] % TSIDE).astype(jnp.float32) + 0.5
    pixel_y = (block_row[:, None] * TSIDE + within[None, :] // TSIDE).astype(jnp.float32) + 0.5
    return (pixel_x, pixel_y)


def composite(arrived, orders, cotangent):
    parts_count = arrived.shape[0]
    ranks_onehot = (
        orders[:, None, :] == jnp.arange(parts_count, dtype=jnp.int32)[None, :, None]
    ).astype(jnp.float32)
    ordered = jnp.einsum("irk,kicp->ircp", ranks_onehot, arrived, precision=lax.Precision.HIGHEST)
    colour = ordered[:, :, :3]
    transmit = ordered[:, :, 3]
    running = jnp.cumprod(transmit, axis=1)
    prefix = jnp.concatenate([jnp.ones_like(running[:, :1]), running[:, :-1]], axis=1)
    rendered = jnp.sum(prefix[:, :, None, :] * colour, axis=1)

    def compose(earlier, later):
        return (earlier[0] * later[0], later[1] + later[0][:, :, None, :] * earlier[1])

    flipped = lax.associative_scan(compose, (transmit[:, ::-1], colour[:, ::-1]), axis=1)
    suffix = flipped[1][:, ::-1]
    behind = jnp.concatenate([suffix[:, 1:], jnp.zeros_like(suffix[:, :1])], axis=1)
    upstream_cot = jnp.transpose(cotangent, (1, 0, 2))
    grad_colour = prefix[:, :, None, :] * upstream_cot[:, None]
    grad_transmit = prefix * jnp.sum(upstream_cot[:, None] * behind, axis=2)
    grad_ordered = jnp.concatenate([grad_colour, grad_transmit[:, :, None, :]], axis=2)
    upstream = jnp.einsum(
        "irk,ircp->kicp", ranks_onehot, grad_ordered, precision=lax.Precision.HIGHEST
    )
    return (jnp.transpose(rendered, (1, 0, 2)), upstream)


def local(geometry, opacity, colours, coverage, gauss_lists, orders, cotangent):
    parts_count = lax.axis_size("dom")
    group_index = lax.axis_index("tile")
    tiles_per = orders.shape[0]
    pixels = cotangent.shape[2]
    params = jnp.concatenate([geometry, opacity[None, :], colours], axis=0)
    gauss_total = params.shape[1]
    tile_ids = coverage[0, 0]
    entries = gauss_lists[0, 0]
    slots_count = tile_ids.shape[0]
    turn_rows = math.gcd(slots_count, 4)
    covered = jnp.sum((tile_ids >= 0).astype(jnp.int32))
    turn_count = (covered + turn_rows - 1) // turn_rows
    pixel_x, pixel_y = pixel_grid(tile_ids, group_index, tiles_per, pixels)
    default = jnp.concatenate(
        [jnp.zeros((3, pixels), jnp.float32), jnp.ones((1, pixels), jnp.float32)], axis=0
    )

    live_all = entries >= 0
    groups_count = lax.axis_size("tile")
    shard = gauss_total // groups_count
    lo_size = 384 if shard % 384 == 0 else shard
    hi_size = gauss_total // lo_size
    safe_index = jnp.where(live_all, entries, 0).reshape(-1)
    hi_pick = (
        safe_index[None, None, :] // lo_size
        == jnp.arange(hi_size, dtype=jnp.int32)[None, :, None]
    ).astype(jnp.float32)
    lo_pick = (
        safe_index[None, :] % lo_size == jnp.arange(lo_size, dtype=jnp.int32)[:, None]
    ).astype(jnp.float32)
    by_row = jnp.einsum(
        "chl,le->che",
        params.reshape(params.shape[0], hi_size, lo_size),
        lo_pick,
        precision=lax.Precision.HIGHEST,
    )
    chosen_all = jnp.sum(by_row * hi_pick, axis=1).reshape((params.shape[0],) + entries.shape)
    live_all_f = live_all.astype(jnp.float32)

    def gather_turn(first_row):
        index_rows = lax.dynamic_slice_in_dim(entries, first_row, turn_rows, 0)
        live = lax.dynamic_slice_in_dim(live_all_f, first_row, turn_rows, 0)
        chosen = lax.dynamic_slice_in_dim(chosen_all, first_row, turn_rows, 1)
        rows_x = lax.dynamic_slice_in_dim(pixel_x, first_row, turn_rows, 0)
        rows_y = lax.dynamic_slice_in_dim(pixel_y, first_row, turn_rows, 0)
        return (index_rows, live, chosen, rows_x, rows_y)

    def forward_turn(turn_index, partial_value):
        first_row = turn_index * turn_rows
        index_rows, live_mask, chosen, rows_x, rows_y = gather_turn(first_row)
        colour, transmit = render(chosen, rows_x, rows_y, live_mask)
        packed = jnp.concatenate([colour, transmit[:, None, :]], axis=1)
        return lax.dynamic_update_slice_in_dim(partial_value, packed, first_row, 0)

    partial_value = lax.fori_loop(
        0, turn_count, forward_turn, jnp.broadcast_to(default, (slots_count, 4, pixels))
    )
    home = lax.axis_index("dom")
    cover_all = lax.all_gather(tile_ids.astype(jnp.float32), "dom", axis=0, tiled=False)
    first_here = jnp.any(cover_all == (home * tiles_per).astype(jnp.float32), axis=1)
    second_here = jnp.any(cover_all == (home * tiles_per + 1).astype(jnp.float32), axis=1)
    target = jnp.where(tile_ids >= 0, tile_ids // tiles_per, parts_count)
    dense = (
        jnp.broadcast_to(default, (parts_count, 4, pixels))
        .at[target]
        .set(partial_value, mode="drop")
    )
    landed = lax.all_to_all(dense, "dom", split_axis=0, concat_axis=0, tiled=True)
    blank = jnp.broadcast_to(default, landed.shape)
    arrived = jnp.stack(
        [
            jnp.where(first_here[:, None, None], landed, blank),
            jnp.where(second_here[:, None, None], landed, blank),
        ],
        axis=1,
    )
    rendered, upstream = composite(arrived, orders, cotangent)
    sent_back = jnp.where(second_here[:, None, None], upstream[:, 1], upstream[:, 0])
    returned = lax.all_to_all(sent_back, "dom", split_axis=0, concat_axis=0, tiled=True)
    slot_grads = jnp.take(returned, jnp.maximum(tile_ids, 0) // tiles_per, axis=0)

    def backward_turn(turn_index, compact):
        first_row = turn_index * turn_rows
        index_rows, live_mask, chosen, rows_x, rows_y = gather_turn(first_row)
        upper_cot = lax.dynamic_slice_in_dim(slot_grads, first_row, turn_rows, 0)
        _, pullback = jax.vjp(lambda values: render(values, rows_x, rows_y, live_mask), chosen)
        grad_chosen = pullback((upper_cot[:, :3], upper_cot[:, 3]))[0]
        return lax.dynamic_update_slice_in_dim(compact, grad_chosen, first_row, 1)

    compact = lax.fori_loop(
        0, turn_count, backward_turn, jnp.zeros(chosen_all.shape, jnp.float32)
    )
    rows_count = params.shape[0]
    flat_index = jnp.where(live_all, entries, -1).reshape(-1)
    values = jnp.where(live_all[None], compact, 0.0).reshape(rows_count, -1)
    hi_index = jnp.where(flat_index >= 0, flat_index // lo_size, -1)
    lo_index = flat_index % lo_size
    spread = values[:, None, :] * (
        hi_index[None, None, :] == jnp.arange(hi_size, dtype=jnp.int32)[None, :, None]
    ).astype(jnp.float32)
    lo_hot = (lo_index[None, :] == jnp.arange(lo_size, dtype=jnp.int32)[:, None]).astype(
        jnp.float32
    )
    placed = jnp.einsum("che,le->chl", spread, lo_hot, precision=lax.Precision.HIGHEST)
    gathered = lax.all_to_all(placed, "tile", split_axis=1, concat_axis=1, tiled=True)
    total = jnp.sum(
        gathered.reshape(rows_count, groups_count, hi_size // groups_count, lo_size), axis=1
    )
    shares = total.reshape(rows_count, shard)
    return (rendered, shares[:5], shares[5], shares[6:])


def solution(mesh):
    placed = (
        P(None, "dom"),
        P("dom"),
        P(None, "dom"),
        P("dom", "tile", None),
        P("dom", "tile", None, None),
        P(("dom", "tile"), None),
        P(None, ("dom", "tile"), None),
    )
    return jax.shard_map(
        local,
        mesh=mesh,
        in_specs=placed,
        out_specs=(
            P(None, ("dom", "tile"), None),
            P(None, ("dom", "tile")),
            P(("dom", "tile")),
            P(None, ("dom", "tile")),
        ),
        check_vma=False,
    )
```

```python
import math

import jax
import jax.numpy as jnp
from jax import lax
from jax.sharding import PartitionSpec as P

TSIDE = 16


def render(params, pixel_x, pixel_y, live_mask):
    centre_x = params[0][:, None, :]
    centre_y = params[1][:, None, :]
    inv_one = jnp.exp(-2.0 * params[2])
    inv_two = jnp.exp(-2.0 * params[3])
    cosine = jnp.cos(params[4])
    sine_angle = jnp.sin(params[4])
    coef_a = (cosine * cosine * inv_one + sine_angle * sine_angle * inv_two)[:, None, :]
    coef_b = (cosine * sine_angle * (inv_one - inv_two))[:, None, :]
    coef_c = (sine_angle * sine_angle * inv_one + cosine * cosine * inv_two)[:, None, :]
    delta_x = pixel_x[:, :, None] - centre_x
    delta_y = pixel_y[:, :, None] - centre_y
    quadratic = (
        coef_a * delta_x * delta_x + 2.0 * coef_b * delta_x * delta_y + coef_c * delta_y * delta_y
    )
    strength = jax.nn.sigmoid(params[5]) * live_mask
    opaque_part = strength[:, None, :] * jnp.exp(-0.5 * quadratic)
    log_keep = jnp.log1p(-opaque_part)
    entries_count = log_keep.shape[2]
    ahead = (
        jnp.arange(entries_count, dtype=jnp.int32)[:, None]
        < jnp.arange(entries_count, dtype=jnp.int32)[None, :]
    ).astype(jnp.float32)
    before = jnp.einsum("kpg,gh->kph", log_keep, ahead, precision=lax.Precision.HIGHEST)
    weight = opaque_part * jnp.exp(before)
    colour = jnp.einsum("kpg,ckg->kcp", weight, params[6:9], precision=lax.Precision.HIGHEST)
    transmit = jnp.exp(jnp.sum(log_keep, axis=2))
    return (colour, transmit)


def pixel_grid(tile_ids, group_index, tiles_per, pixels):
    safe_ids = jnp.maximum(tile_ids, 0)
    block_row = safe_ids // tiles_per
    column = group_index * tiles_per + safe_ids % tiles_per
    within = jnp.arange(pixels, dtype=jnp.int32)
    pixel_x = (column[:, None] * TSIDE + within[None, :] % TSIDE).astype(jnp.float32) + 0.5
    pixel_y = (block_row[:, None] * TSIDE + within[None, :] // TSIDE).astype(jnp.float32) + 0.5
    return (pixel_x, pixel_y)


def composite(arrived, orders, cotangent):
    parts_count = arrived.shape[0]
    ranks_onehot = (
        orders[:, None, :] == jnp.arange(parts_count, dtype=jnp.int32)[None, :, None]
    ).astype(jnp.float32)
    ordered = jnp.einsum("irk,kicp->ircp", ranks_onehot, arrived, precision=lax.Precision.HIGHEST)
    colour = ordered[:, :, :3]
    transmit = ordered[:, :, 3]
    running = jnp.cumprod(transmit, axis=1)
    prefix = jnp.concatenate([jnp.ones_like(running[:, :1]), running[:, :-1]], axis=1)
    rendered = jnp.sum(prefix[:, :, None, :] * colour, axis=1)

    def compose(earlier, later):
        return (earlier[0] * later[0], later[1] + later[0][:, :, None, :] * earlier[1])

    flipped = lax.associative_scan(compose, (transmit[:, ::-1], colour[:, ::-1]), axis=1)
    suffix = flipped[1][:, ::-1]
    behind = jnp.concatenate([suffix[:, 1:], jnp.zeros_like(suffix[:, :1])], axis=1)
    upstream_cot = jnp.transpose(cotangent, (1, 0, 2))
    grad_colour = prefix[:, :, None, :] * upstream_cot[:, None]
    grad_transmit = prefix * jnp.sum(upstream_cot[:, None] * behind, axis=2)
    grad_ordered = jnp.concatenate([grad_colour, grad_transmit[:, :, None, :]], axis=2)
    upstream = jnp.einsum(
        "irk,ircp->kicp", ranks_onehot, grad_ordered, precision=lax.Precision.HIGHEST
    )
    return (jnp.transpose(rendered, (1, 0, 2)), upstream)


def local(geometry, opacity, colours, coverage, gauss_lists, orders, cotangent):
    parts_count = lax.axis_size("dom")
    group_index = lax.axis_index("tile")
    tiles_per = orders.shape[0]
    pixels = cotangent.shape[2]
    params = jnp.concatenate([geometry, opacity[None, :], colours], axis=0)
    gauss_total = params.shape[1]
    tile_ids = coverage[0, 0]
    entries = gauss_lists[0, 0]
    slots_count = tile_ids.shape[0]
    turn_rows = math.gcd(slots_count, 4)
    covered = jnp.sum((tile_ids >= 0).astype(jnp.int32))
    turn_count = (covered + turn_rows - 1) // turn_rows
    pixel_x, pixel_y = pixel_grid(tile_ids, group_index, tiles_per, pixels)
    default = jnp.concatenate(
        [jnp.zeros((3, pixels), jnp.float32), jnp.ones((1, pixels), jnp.float32)], axis=0
    )

    live_all = entries >= 0
    groups_count = lax.axis_size("tile")
    shard = gauss_total // groups_count
    lo_size = 384 if shard % 384 == 0 else shard
    hi_size = gauss_total // lo_size
    safe_index = jnp.where(live_all, entries, 0).reshape(-1)
    hi_pick = (
        safe_index[None, None, :] // lo_size
        == jnp.arange(hi_size, dtype=jnp.int32)[None, :, None]
    ).astype(jnp.float32)
    lo_pick = (
        safe_index[None, :] % lo_size == jnp.arange(lo_size, dtype=jnp.int32)[:, None]
    ).astype(jnp.float32)
    by_row = jnp.einsum(
        "chl,le->che",
        params.reshape(params.shape[0], hi_size, lo_size),
        lo_pick,
        precision=lax.Precision.HIGHEST,
    )
    chosen_all = jnp.sum(by_row * hi_pick, axis=1).reshape((params.shape[0],) + entries.shape)
    live_all_f = live_all.astype(jnp.float32)

    def gather_turn(first_row):
        index_rows = lax.dynamic_slice_in_dim(entries, first_row, turn_rows, 0)
        live = lax.dynamic_slice_in_dim(live_all_f, first_row, turn_rows, 0)
        chosen = lax.dynamic_slice_in_dim(chosen_all, first_row, turn_rows, 1)
        rows_x = lax.dynamic_slice_in_dim(pixel_x, first_row, turn_rows, 0)
        rows_y = lax.dynamic_slice_in_dim(pixel_y, first_row, turn_rows, 0)
        return (index_rows, live, chosen, rows_x, rows_y)

    def forward_turn(turn_index, partial_value):
        first_row = turn_index * turn_rows
        index_rows, live_mask, chosen, rows_x, rows_y = gather_turn(first_row)
        colour, transmit = render(chosen, rows_x, rows_y, live_mask)
        packed = jnp.concatenate([colour, transmit[:, None, :]], axis=1)
        return lax.dynamic_update_slice_in_dim(partial_value, packed, first_row, 0)

    partial_value = lax.fori_loop(
        0, turn_count, forward_turn, jnp.broadcast_to(default, (slots_count, 4, pixels))
    )
    target = jnp.where(tile_ids >= 0, tile_ids // tiles_per, parts_count)
    dense = (
        jnp.broadcast_to(default, (parts_count, 4, pixels))
        .at[target]
        .set(partial_value, mode="drop")
    )
    offset = (
        jnp.zeros((parts_count,), jnp.float32)
        .at[target]
        .set((tile_ids % tiles_per).astype(jnp.float32), mode="drop")
    )
    tag_width = 128
    payload = jnp.concatenate(
        [
            dense.reshape(parts_count, 4 * pixels),
            jnp.broadcast_to(offset[:, None], (parts_count, tag_width)),
        ],
        axis=1,
    )
    landed = lax.all_to_all(payload, "dom", split_axis=0, concat_axis=0, tiled=True)
    second_here = landed[:, 4 * pixels] > 0.5
    landed = landed[:, : 4 * pixels].reshape(parts_count, 4, pixels)
    blank = jnp.broadcast_to(default, landed.shape)
    arrived = jnp.stack(
        [
            jnp.where(second_here[:, None, None], blank, landed),
            jnp.where(second_here[:, None, None], landed, blank),
        ],
        axis=1,
    )
    rendered, upstream = composite(arrived, orders, cotangent)
    sent_back = jnp.where(second_here[:, None, None], upstream[:, 1], upstream[:, 0])
    returned = lax.all_to_all(sent_back, "dom", split_axis=0, concat_axis=0, tiled=True)
    slot_grads = jnp.take(returned, jnp.maximum(tile_ids, 0) // tiles_per, axis=0)

    def backward_turn(turn_index, compact):
        first_row = turn_index * turn_rows
        index_rows, live_mask, chosen, rows_x, rows_y = gather_turn(first_row)
        upper_cot = lax.dynamic_slice_in_dim(slot_grads, first_row, turn_rows, 0)
        _, pullback = jax.vjp(lambda values: render(values, rows_x, rows_y, live_mask), chosen)
        grad_chosen = pullback((upper_cot[:, :3], upper_cot[:, 3]))[0]
        return lax.dynamic_update_slice_in_dim(compact, grad_chosen, first_row, 1)

    compact = lax.fori_loop(
        0, turn_count, backward_turn, jnp.zeros(chosen_all.shape, jnp.float32)
    )
    rows_count = params.shape[0]
    flat_index = jnp.where(live_all, entries, -1).reshape(-1)
    values = jnp.where(live_all[None], compact, 0.0).reshape(rows_count, -1)
    hi_index = jnp.where(flat_index >= 0, flat_index // lo_size, -1)
    lo_index = flat_index % lo_size
    spread = values[:, None, :] * (
        hi_index[None, None, :] == jnp.arange(hi_size, dtype=jnp.int32)[None, :, None]
    ).astype(jnp.float32)
    lo_hot = (lo_index[None, :] == jnp.arange(lo_size, dtype=jnp.int32)[:, None]).astype(
        jnp.float32
    )
    placed = jnp.einsum("che,le->chl", spread, lo_hot, precision=lax.Precision.HIGHEST)
    gathered = lax.all_to_all(placed, "tile", split_axis=1, concat_axis=1, tiled=True)
    total = jnp.sum(
        gathered.reshape(rows_count, groups_count, hi_size // groups_count, lo_size), axis=1
    )
    shares = total.reshape(rows_count, shard)
    return (rendered, shares[:5], shares[5], shares[6:])


def solution(mesh):
    placed = (
        P(None, "dom"),
        P("dom"),
        P(None, "dom"),
        P("dom", "tile", None),
        P("dom", "tile", None, None),
        P(("dom", "tile"), None),
        P(None, ("dom", "tile"), None),
    )
    return jax.shard_map(
        local,
        mesh=mesh,
        in_specs=placed,
        out_specs=(
            P(None, ("dom", "tile"), None),
            P(None, ("dom", "tile")),
            P(("dom", "tile")),
            P(None, ("dom", "tile")),
        ),
        check_vma=False,
    )
```

```python
import math

import jax
import jax.numpy as jnp
from jax import lax
from jax.sharding import PartitionSpec as P

TSIDE = 16


def render(params, pixel_x, pixel_y, live_mask):
    centre_x = params[0][:, None, :]
    centre_y = params[1][:, None, :]
    inv_one = jnp.exp(-2.0 * params[2])
    inv_two = jnp.exp(-2.0 * params[3])
    cosine = jnp.cos(params[4])
    sine_angle = jnp.sin(params[4])
    coef_a = (cosine * cosine * inv_one + sine_angle * sine_angle * inv_two)[:, None, :]
    coef_b = (cosine * sine_angle * (inv_one - inv_two))[:, None, :]
    coef_c = (sine_angle * sine_angle * inv_one + cosine * cosine * inv_two)[:, None, :]
    delta_x = pixel_x[:, :, None] - centre_x
    delta_y = pixel_y[:, :, None] - centre_y
    quadratic = (
        coef_a * delta_x * delta_x + 2.0 * coef_b * delta_x * delta_y + coef_c * delta_y * delta_y
    )
    strength = jax.nn.sigmoid(params[5]) * live_mask
    opaque_part = strength[:, None, :] * jnp.exp(-0.5 * quadratic)
    log_keep = jnp.log1p(-opaque_part)
    entries_count = log_keep.shape[2]
    ahead = (
        jnp.arange(entries_count, dtype=jnp.int32)[:, None]
        < jnp.arange(entries_count, dtype=jnp.int32)[None, :]
    ).astype(jnp.float32)
    before = jnp.einsum("kpg,gh->kph", log_keep, ahead, precision=lax.Precision.HIGHEST)
    weight = opaque_part * jnp.exp(before)
    colour = jnp.einsum("kpg,ckg->kcp", weight, params[6:9], precision=lax.Precision.HIGHEST)
    transmit = jnp.exp(jnp.sum(log_keep, axis=2))
    return (colour, transmit)


def pixel_grid(tile_ids, group_index, tiles_per, pixels):
    safe_ids = jnp.maximum(tile_ids, 0)
    block_row = safe_ids // tiles_per
    column = group_index * tiles_per + safe_ids % tiles_per
    within = jnp.arange(pixels, dtype=jnp.int32)
    pixel_x = (column[:, None] * TSIDE + within[None, :] % TSIDE).astype(jnp.float32) + 0.5
    pixel_y = (block_row[:, None] * TSIDE + within[None, :] // TSIDE).astype(jnp.float32) + 0.5
    return (pixel_x, pixel_y)


def composite(arrived, orders, cotangent):
    parts_count = arrived.shape[0]
    ranks_onehot = (
        orders[:, None, :] == jnp.arange(parts_count, dtype=jnp.int32)[None, :, None]
    ).astype(jnp.float32)
    ordered = jnp.einsum("irk,kicp->ircp", ranks_onehot, arrived, precision=lax.Precision.HIGHEST)
    colour = ordered[:, :, :3]
    transmit = ordered[:, :, 3]
    running = jnp.cumprod(transmit, axis=1)
    prefix = jnp.concatenate([jnp.ones_like(running[:, :1]), running[:, :-1]], axis=1)
    rendered = jnp.sum(prefix[:, :, None, :] * colour, axis=1)

    def compose(earlier, later):
        return (earlier[0] * later[0], later[1] + later[0][:, :, None, :] * earlier[1])

    flipped = lax.associative_scan(compose, (transmit[:, ::-1], colour[:, ::-1]), axis=1)
    suffix = flipped[1][:, ::-1]
    behind = jnp.concatenate([suffix[:, 1:], jnp.zeros_like(suffix[:, :1])], axis=1)
    upstream_cot = jnp.transpose(cotangent, (1, 0, 2))
    grad_colour = prefix[:, :, None, :] * upstream_cot[:, None]
    grad_transmit = prefix * jnp.sum(upstream_cot[:, None] * behind, axis=2)
    grad_ordered = jnp.concatenate([grad_colour, grad_transmit[:, :, None, :]], axis=2)
    upstream = jnp.einsum(
        "irk,ircp->kicp", ranks_onehot, grad_ordered, precision=lax.Precision.HIGHEST
    )
    return (jnp.transpose(rendered, (1, 0, 2)), upstream)


def local(geometry, opacity, colours, coverage, gauss_lists, orders, cotangent):
    parts_count = lax.axis_size("dom")
    group_index = lax.axis_index("tile")
    tiles_per = orders.shape[0]
    pixels = cotangent.shape[2]
    params = jnp.concatenate([geometry, opacity[None, :], colours], axis=0)
    gauss_total = params.shape[1]
    tile_ids = coverage[0, 0]
    entries = gauss_lists[0, 0]
    slots_count = tile_ids.shape[0]
    turn_rows = math.gcd(slots_count, 4)
    covered = jnp.sum((tile_ids >= 0).astype(jnp.int32))
    turn_count = (covered + turn_rows - 1) // turn_rows
    pixel_x, pixel_y = pixel_grid(tile_ids, group_index, tiles_per, pixels)
    default = jnp.concatenate(
        [jnp.zeros((3, pixels), jnp.float32), jnp.ones((1, pixels), jnp.float32)], axis=0
    )

    live_all = entries >= 0
    groups_count = lax.axis_size("tile")
    shard = gauss_total // groups_count
    lo_size = 384 if shard % 384 == 0 else shard
    hi_size = gauss_total // lo_size
    safe_index = jnp.where(live_all, entries, 0).reshape(-1)
    hi_pick = (
        safe_index[None, None, :] // lo_size
        == jnp.arange(hi_size, dtype=jnp.int32)[:, None, None]
    ).astype(jnp.float32)
    lo_pick = (
        safe_index[None, :] % lo_size == jnp.arange(lo_size, dtype=jnp.int32)[:, None]
    ).astype(jnp.float32)
    by_row = jnp.einsum(
        "chl,le->hce",
        params.reshape(params.shape[0], hi_size, lo_size),
        lo_pick,
        precision=lax.Precision.HIGHEST,
    )
    chosen_all = jnp.sum(by_row * hi_pick, axis=0).reshape((params.shape[0],) + entries.shape)
    live_all_f = live_all.astype(jnp.float32)

    def gather_turn(first_row):
        index_rows = lax.dynamic_slice_in_dim(entries, first_row, turn_rows, 0)
        live = lax.dynamic_slice_in_dim(live_all_f, first_row, turn_rows, 0)
        chosen = lax.dynamic_slice_in_dim(chosen_all, first_row, turn_rows, 1)
        rows_x = lax.dynamic_slice_in_dim(pixel_x, first_row, turn_rows, 0)
        rows_y = lax.dynamic_slice_in_dim(pixel_y, first_row, turn_rows, 0)
        return (index_rows, live, chosen, rows_x, rows_y)

    def forward_turn(turn_index, partial_value):
        first_row = turn_index * turn_rows
        index_rows, live_mask, chosen, rows_x, rows_y = gather_turn(first_row)
        colour, transmit = render(chosen, rows_x, rows_y, live_mask)
        packed = jnp.concatenate([colour, transmit[:, None, :]], axis=1)
        return lax.dynamic_update_slice_in_dim(partial_value, packed, first_row, 0)

    partial_value = lax.fori_loop(
        0, turn_count, forward_turn, jnp.broadcast_to(default, (slots_count, 4, pixels))
    )
    target = jnp.where(tile_ids >= 0, tile_ids // tiles_per, parts_count)
    dense = (
        jnp.broadcast_to(default, (parts_count, 4, pixels))
        .at[target]
        .set(partial_value, mode="drop")
    )
    offset = (
        jnp.zeros((parts_count,), jnp.float32)
        .at[target]
        .set((tile_ids % tiles_per).astype(jnp.float32), mode="drop")
    )
    tag_width = 128
    payload = jnp.concatenate(
        [
            dense.reshape(parts_count, 4 * pixels),
            jnp.broadcast_to(offset[:, None], (parts_count, tag_width)),
        ],
        axis=1,
    )
    landed = lax.all_to_all(payload, "dom", split_axis=0, concat_axis=0, tiled=True)
    second_here = landed[:, 4 * pixels] > 0.5
    landed = landed[:, : 4 * pixels].reshape(parts_count, 4, pixels)
    blank = jnp.broadcast_to(default, landed.shape)
    arrived = jnp.stack(
        [
            jnp.where(second_here[:, None, None], blank, landed),
            jnp.where(second_here[:, None, None], landed, blank),
        ],
        axis=1,
    )
    rendered, upstream = composite(arrived, orders, cotangent)
    sent_back = jnp.where(second_here[:, None, None], upstream[:, 1], upstream[:, 0])
    returned = lax.all_to_all(sent_back, "dom", split_axis=0, concat_axis=0, tiled=True)
    slot_grads = jnp.take(returned, jnp.maximum(tile_ids, 0) // tiles_per, axis=0)

    def backward_turn(turn_index, compact):
        first_row = turn_index * turn_rows
        index_rows, live_mask, chosen, rows_x, rows_y = gather_turn(first_row)
        upper_cot = lax.dynamic_slice_in_dim(slot_grads, first_row, turn_rows, 0)
        _, pullback = jax.vjp(lambda values: render(values, rows_x, rows_y, live_mask), chosen)
        grad_chosen = pullback((upper_cot[:, :3], upper_cot[:, 3]))[0]
        return lax.dynamic_update_slice_in_dim(compact, grad_chosen, first_row, 1)

    compact = lax.fori_loop(
        0, turn_count, backward_turn, jnp.zeros(chosen_all.shape, jnp.float32)
    )
    rows_count = params.shape[0]
    flat_index = jnp.where(live_all, entries, -1).reshape(-1)
    values = jnp.where(live_all[None], compact, 0.0).reshape(rows_count, -1)
    hi_index = jnp.where(flat_index >= 0, flat_index // lo_size, -1)
    lo_index = flat_index % lo_size
    spread = values[:, None, :] * (
        hi_index[None, None, :] == jnp.arange(hi_size, dtype=jnp.int32)[None, :, None]
    ).astype(jnp.float32)
    lo_hot = (lo_index[None, :] == jnp.arange(lo_size, dtype=jnp.int32)[:, None]).astype(
        jnp.float32
    )
    placed = jnp.einsum("che,le->chl", spread, lo_hot, precision=lax.Precision.HIGHEST)
    gathered = lax.all_to_all(placed, "tile", split_axis=1, concat_axis=1, tiled=True)
    total = jnp.sum(
        gathered.reshape(rows_count, groups_count, hi_size // groups_count, lo_size), axis=1
    )
    shares = total.reshape(rows_count, shard)
    return (rendered, shares[:5], shares[5], shares[6:])


def solution(mesh):
    placed = (
        P(None, "dom"),
        P("dom"),
        P(None, "dom"),
        P("dom", "tile", None),
        P("dom", "tile", None, None),
        P(("dom", "tile"), None),
        P(None, ("dom", "tile"), None),
    )
    return jax.shard_map(
        local,
        mesh=mesh,
        in_specs=placed,
        out_specs=(
            P(None, ("dom", "tile"), None),
            P(None, ("dom", "tile")),
            P(("dom", "tile")),
            P(None, ("dom", "tile")),
        ),
        check_vma=False,
    )
```

```python
import math

import jax
import jax.numpy as jnp
from jax import lax
from jax.sharding import PartitionSpec as P

TSIDE = 16


def render(params, pixel_x, pixel_y, live_mask):
    centre_x = params[0][:, None, :]
    centre_y = params[1][:, None, :]
    inv_one = jnp.exp(-2.0 * params[2])
    inv_two = jnp.exp(-2.0 * params[3])
    cosine = jnp.cos(params[4])
    sine_angle = jnp.sin(params[4])
    coef_a = (cosine * cosine * inv_one + sine_angle * sine_angle * inv_two)[:, None, :]
    coef_b = (cosine * sine_angle * (inv_one - inv_two))[:, None, :]
    coef_c = (sine_angle * sine_angle * inv_one + cosine * cosine * inv_two)[:, None, :]
    delta_x = pixel_x[:, :, None] - centre_x
    delta_y = pixel_y[:, :, None] - centre_y
    quadratic = (
        coef_a * delta_x * delta_x + 2.0 * coef_b * delta_x * delta_y + coef_c * delta_y * delta_y
    )
    strength = jax.nn.sigmoid(params[5]) * live_mask
    opaque_part = strength[:, None, :] * jnp.exp(-0.5 * quadratic)
    log_keep = jnp.log1p(-opaque_part)
    entries_count = log_keep.shape[2]
    ahead = (
        jnp.arange(entries_count, dtype=jnp.int32)[:, None]
        < jnp.arange(entries_count, dtype=jnp.int32)[None, :]
    ).astype(jnp.float32)
    before = jnp.einsum("kpg,gh->kph", log_keep, ahead, precision=lax.Precision.HIGHEST)
    weight = opaque_part * jnp.exp(before)
    colour = jnp.einsum("kpg,ckg->kcp", weight, params[6:9], precision=lax.Precision.HIGHEST)
    transmit = jnp.exp(jnp.sum(log_keep, axis=2))
    return (colour, transmit)


def pixel_grid(tile_ids, group_index, tiles_per, pixels):
    safe_ids = jnp.maximum(tile_ids, 0)
    block_row = safe_ids // tiles_per
    column = group_index * tiles_per + safe_ids % tiles_per
    within = jnp.arange(pixels, dtype=jnp.int32)
    pixel_x = (column[:, None] * TSIDE + within[None, :] % TSIDE).astype(jnp.float32) + 0.5
    pixel_y = (block_row[:, None] * TSIDE + within[None, :] // TSIDE).astype(jnp.float32) + 0.5
    return (pixel_x, pixel_y)


def composite(arrived, orders, cotangent):
    parts_count = arrived.shape[0]
    ranks_onehot = (
        orders[:, None, :] == jnp.arange(parts_count, dtype=jnp.int32)[None, :, None]
    ).astype(jnp.float32)
    ordered = jnp.einsum("irk,kicp->ircp", ranks_onehot, arrived, precision=lax.Precision.HIGHEST)
    colour = ordered[:, :, :3]
    transmit = ordered[:, :, 3]
    ahead = (
        jnp.arange(parts_count, dtype=jnp.int32)[:, None]
        < jnp.arange(parts_count, dtype=jnp.int32)[None, :]
    ).astype(jnp.float32)
    prefix = jnp.exp(
        jnp.einsum("iqp,qr->irp", jnp.log(transmit), ahead, precision=lax.Precision.HIGHEST)
    )
    rendered = jnp.sum(prefix[:, :, None, :] * colour, axis=1)
    upstream_cot = jnp.transpose(cotangent, (1, 0, 2))
    grad_colour = prefix[:, :, None, :] * upstream_cot[:, None]
    weighted = prefix * jnp.sum(upstream_cot[:, None] * colour, axis=2)
    behind = jnp.einsum("iqp,rq->irp", weighted, ahead, precision=lax.Precision.HIGHEST)
    grad_transmit = behind / transmit
    grad_ordered = jnp.concatenate([grad_colour, grad_transmit[:, :, None, :]], axis=2)
    upstream = jnp.einsum(
        "irk,ircp->kicp", ranks_onehot, grad_ordered, precision=lax.Precision.HIGHEST
    )
    return (jnp.transpose(rendered, (1, 0, 2)), upstream)


def local(geometry, opacity, colours, coverage, gauss_lists, orders, cotangent):
    parts_count = lax.axis_size("dom")
    group_index = lax.axis_index("tile")
    tiles_per = orders.shape[0]
    pixels = cotangent.shape[2]
    params = jnp.concatenate([geometry, opacity[None, :], colours], axis=0)
    gauss_total = params.shape[1]
    tile_ids = coverage[0, 0]
    entries = gauss_lists[0, 0]
    slots_count = tile_ids.shape[0]
    turn_rows = math.gcd(slots_count, 4)
    covered = jnp.sum((tile_ids >= 0).astype(jnp.int32))
    turn_count = (covered + turn_rows - 1) // turn_rows
    pixel_x, pixel_y = pixel_grid(tile_ids, group_index, tiles_per, pixels)
    default = jnp.concatenate(
        [jnp.zeros((3, pixels), jnp.float32), jnp.ones((1, pixels), jnp.float32)], axis=0
    )

    live_all = entries >= 0
    groups_count = lax.axis_size("tile")
    shard = gauss_total // groups_count
    lo_size = 384 if shard % 384 == 0 else shard
    hi_size = gauss_total // lo_size
    safe_index = jnp.where(live_all, entries, 0).reshape(-1)
    hi_pick = (
        safe_index[None, None, :] // lo_size
        == jnp.arange(hi_size, dtype=jnp.int32)[:, None, None]
    ).astype(jnp.float32)
    lo_pick = (
        safe_index[None, :] % lo_size == jnp.arange(lo_size, dtype=jnp.int32)[:, None]
    ).astype(jnp.float32)
    by_row = jnp.einsum(
        "chl,le->hce",
        params.reshape(params.shape[0], hi_size, lo_size),
        lo_pick,
        precision=lax.Precision.HIGHEST,
    )
    chosen_all = jnp.sum(by_row * hi_pick, axis=0).reshape((params.shape[0],) + entries.shape)
    live_all_f = live_all.astype(jnp.float32)

    def gather_turn(first_row):
        index_rows = lax.dynamic_slice_in_dim(entries, first_row, turn_rows, 0)
        live = lax.dynamic_slice_in_dim(live_all_f, first_row, turn_rows, 0)
        chosen = lax.dynamic_slice_in_dim(chosen_all, first_row, turn_rows, 1)
        rows_x = lax.dynamic_slice_in_dim(pixel_x, first_row, turn_rows, 0)
        rows_y = lax.dynamic_slice_in_dim(pixel_y, first_row, turn_rows, 0)
        return (index_rows, live, chosen, rows_x, rows_y)

    def forward_turn(turn_index, partial_value):
        first_row = turn_index * turn_rows
        index_rows, live_mask, chosen, rows_x, rows_y = gather_turn(first_row)
        colour, transmit = render(chosen, rows_x, rows_y, live_mask)
        packed = jnp.concatenate([colour, transmit[:, None, :]], axis=1)
        return lax.dynamic_update_slice_in_dim(partial_value, packed, first_row, 0)

    partial_value = lax.fori_loop(
        0, turn_count, forward_turn, jnp.broadcast_to(default, (slots_count, 4, pixels))
    )
    target = jnp.where(tile_ids >= 0, tile_ids // tiles_per, parts_count)
    dense = (
        jnp.broadcast_to(default, (parts_count, 4, pixels))
        .at[target]
        .set(partial_value, mode="drop")
    )
    offset = (
        jnp.zeros((parts_count,), jnp.float32)
        .at[target]
        .set((tile_ids % tiles_per).astype(jnp.float32), mode="drop")
    )
    tag_width = 128
    payload = jnp.concatenate(
        [
            dense.reshape(parts_count, 4 * pixels),
            jnp.broadcast_to(offset[:, None], (parts_count, tag_width)),
        ],
        axis=1,
    )
    landed = lax.all_to_all(payload, "dom", split_axis=0, concat_axis=0, tiled=True)
    second_here = landed[:, 4 * pixels] > 0.5
    landed = landed[:, : 4 * pixels].reshape(parts_count, 4, pixels)
    blank = jnp.broadcast_to(default, landed.shape)
    arrived = jnp.stack(
        [
            jnp.where(second_here[:, None, None], blank, landed),
            jnp.where(second_here[:, None, None], landed, blank),
        ],
        axis=1,
    )
    rendered, upstream = composite(arrived, orders, cotangent)
    sent_back = jnp.where(second_here[:, None, None], upstream[:, 1], upstream[:, 0])
    returned = lax.all_to_all(sent_back, "dom", split_axis=0, concat_axis=0, tiled=True)
    slot_grads = jnp.take(returned, jnp.maximum(tile_ids, 0) // tiles_per, axis=0)

    def backward_turn(turn_index, compact):
        first_row = turn_index * turn_rows
        index_rows, live_mask, chosen, rows_x, rows_y = gather_turn(first_row)
        upper_cot = lax.dynamic_slice_in_dim(slot_grads, first_row, turn_rows, 0)
        _, pullback = jax.vjp(lambda values: render(values, rows_x, rows_y, live_mask), chosen)
        grad_chosen = pullback((upper_cot[:, :3], upper_cot[:, 3]))[0]
        return lax.dynamic_update_slice_in_dim(compact, grad_chosen, first_row, 1)

    compact = lax.fori_loop(
        0, turn_count, backward_turn, jnp.zeros(chosen_all.shape, jnp.float32)
    )
    rows_count = params.shape[0]
    flat_index = jnp.where(live_all, entries, -1).reshape(-1)
    values = jnp.where(live_all[None], compact, 0.0).reshape(rows_count, -1)
    hi_index = jnp.where(flat_index >= 0, flat_index // lo_size, -1)
    lo_index = flat_index % lo_size
    spread = values[:, None, :] * (
        hi_index[None, None, :] == jnp.arange(hi_size, dtype=jnp.int32)[None, :, None]
    ).astype(jnp.float32)
    lo_hot = (lo_index[None, :] == jnp.arange(lo_size, dtype=jnp.int32)[:, None]).astype(
        jnp.float32
    )
    placed = jnp.einsum("che,le->chl", spread, lo_hot, precision=lax.Precision.HIGH)
    gathered = lax.all_to_all(placed, "tile", split_axis=1, concat_axis=1, tiled=True)
    total = jnp.sum(
        gathered.reshape(rows_count, groups_count, hi_size // groups_count, lo_size), axis=1
    )
    shares = total.reshape(rows_count, shard)
    return (rendered, shares[:5], shares[5], shares[6:])


def solution(mesh):
    placed = (
        P(None, "dom"),
        P("dom"),
        P(None, "dom"),
        P("dom", "tile", None),
        P("dom", "tile", None, None),
        P(("dom", "tile"), None),
        P(None, ("dom", "tile"), None),
    )
    return jax.shard_map(
        local,
        mesh=mesh,
        in_specs=placed,
        out_specs=(
            P(None, ("dom", "tile"), None),
            P(None, ("dom", "tile")),
            P(("dom", "tile")),
            P(None, ("dom", "tile")),
        ),
        check_vma=False,
    )
```

```python
import math

import jax
import jax.numpy as jnp
from jax import lax
from jax.sharding import PartitionSpec as P

TSIDE = 16


def render(params, pixel_x, pixel_y, live_mask):
    centre_x = params[0][:, None, :]
    centre_y = params[1][:, None, :]
    inv_one = jnp.exp(-2.0 * params[2])
    inv_two = jnp.exp(-2.0 * params[3])
    cosine = jnp.cos(params[4])
    sine_angle = jnp.sin(params[4])
    coef_a = (cosine * cosine * inv_one + sine_angle * sine_angle * inv_two)[:, None, :]
    coef_b = (cosine * sine_angle * (inv_one - inv_two))[:, None, :]
    coef_c = (sine_angle * sine_angle * inv_one + cosine * cosine * inv_two)[:, None, :]
    delta_x = pixel_x[:, :, None] - centre_x
    delta_y = pixel_y[:, :, None] - centre_y
    quadratic = (
        coef_a * delta_x * delta_x + 2.0 * coef_b * delta_x * delta_y + coef_c * delta_y * delta_y
    )
    strength = jax.nn.sigmoid(params[5]) * live_mask
    opaque_part = strength[:, None, :] * jnp.exp(-0.5 * quadratic)
    log_keep = jnp.log1p(-opaque_part)
    entries_count = log_keep.shape[2]
    ahead = (
        jnp.arange(entries_count, dtype=jnp.int32)[:, None]
        < jnp.arange(entries_count, dtype=jnp.int32)[None, :]
    ).astype(jnp.float32)
    before = jnp.einsum("kpg,gh->kph", log_keep, ahead, precision=lax.Precision.HIGHEST)
    weight = opaque_part * jnp.exp(before)
    colour = jnp.einsum("kpg,ckg->kcp", weight, params[6:9], precision=lax.Precision.HIGHEST)
    transmit = jnp.exp(jnp.sum(log_keep, axis=2))
    return (colour, transmit)


def pixel_grid(tile_ids, group_index, tiles_per, pixels):
    safe_ids = jnp.maximum(tile_ids, 0)
    block_row = safe_ids // tiles_per
    column = group_index * tiles_per + safe_ids % tiles_per
    within = jnp.arange(pixels, dtype=jnp.int32)
    pixel_x = (column[:, None] * TSIDE + within[None, :] % TSIDE).astype(jnp.float32) + 0.5
    pixel_y = (block_row[:, None] * TSIDE + within[None, :] // TSIDE).astype(jnp.float32) + 0.5
    return (pixel_x, pixel_y)


def composite(arrived, orders, cotangent):
    parts_count = arrived.shape[0]
    ranks_onehot = (
        orders[:, None, :] == jnp.arange(parts_count, dtype=jnp.int32)[None, :, None]
    ).astype(jnp.float32)
    ordered = jnp.einsum("irk,kicp->ircp", ranks_onehot, arrived, precision=lax.Precision.HIGHEST)
    colour = ordered[:, :, :3]
    transmit = ordered[:, :, 3]
    ahead = (
        jnp.arange(parts_count, dtype=jnp.int32)[:, None]
        < jnp.arange(parts_count, dtype=jnp.int32)[None, :]
    ).astype(jnp.float32)
    prefix = jnp.exp(
        jnp.einsum("iqp,qr->irp", jnp.log(transmit), ahead, precision=lax.Precision.HIGHEST)
    )
    rendered = jnp.sum(prefix[:, :, None, :] * colour, axis=1)
    upstream_cot = jnp.transpose(cotangent, (1, 0, 2))
    grad_colour = prefix[:, :, None, :] * upstream_cot[:, None]
    weighted = prefix * jnp.sum(upstream_cot[:, None] * colour, axis=2)
    behind = jnp.einsum("iqp,rq->irp", weighted, ahead, precision=lax.Precision.HIGHEST)
    grad_transmit = behind / transmit
    grad_ordered = jnp.concatenate([grad_colour, grad_transmit[:, :, None, :]], axis=2)
    upstream = jnp.einsum(
        "irk,ircp->kicp", ranks_onehot, grad_ordered, precision=lax.Precision.HIGHEST
    )
    return (jnp.transpose(rendered, (1, 0, 2)), upstream)


def local(geometry, opacity, colours, coverage, gauss_lists, orders, cotangent):
    parts_count = lax.axis_size("dom")
    group_index = lax.axis_index("tile")
    tiles_per = orders.shape[0]
    pixels = cotangent.shape[2]
    params = jnp.concatenate([geometry, opacity[None, :], colours], axis=0)
    gauss_total = params.shape[1]
    tile_ids = coverage[0, 0]
    entries = gauss_lists[0, 0]
    slots_count = tile_ids.shape[0]
    turn_rows = math.gcd(slots_count, 4)
    covered = jnp.sum((tile_ids >= 0).astype(jnp.int32))
    turn_count = (covered + turn_rows - 1) // turn_rows
    pixel_x, pixel_y = pixel_grid(tile_ids, group_index, tiles_per, pixels)
    default = jnp.concatenate(
        [jnp.zeros((3, pixels), jnp.float32), jnp.ones((1, pixels), jnp.float32)], axis=0
    )

    live_all = entries >= 0
    groups_count = lax.axis_size("tile")
    shard = gauss_total // groups_count
    lo_size = 384 if shard % 384 == 0 else shard
    hi_size = gauss_total // lo_size
    safe_index = jnp.where(live_all, entries, 0).reshape(-1)
    hi_pick = (
        safe_index[None, None, :] // lo_size
        == jnp.arange(hi_size, dtype=jnp.int32)[:, None, None]
    ).astype(jnp.float32)
    lo_pick = (
        safe_index[None, :] % lo_size == jnp.arange(lo_size, dtype=jnp.int32)[:, None]
    ).astype(jnp.float32)
    by_row = jnp.einsum(
        "chl,le->hce",
        params.reshape(params.shape[0], hi_size, lo_size),
        lo_pick,
        precision=lax.Precision.HIGHEST,
    )
    chosen_all = jnp.sum(by_row * hi_pick, axis=0).reshape((params.shape[0],) + entries.shape)
    live_all_f = live_all.astype(jnp.float32)

    def gather_turn(first_row):
        index_rows = lax.dynamic_slice_in_dim(entries, first_row, turn_rows, 0)
        live = lax.dynamic_slice_in_dim(live_all_f, first_row, turn_rows, 0)
        chosen = lax.dynamic_slice_in_dim(chosen_all, first_row, turn_rows, 1)
        rows_x = lax.dynamic_slice_in_dim(pixel_x, first_row, turn_rows, 0)
        rows_y = lax.dynamic_slice_in_dim(pixel_y, first_row, turn_rows, 0)
        return (index_rows, live, chosen, rows_x, rows_y)

    def forward_turn(turn_index, partial_value):
        first_row = turn_index * turn_rows
        index_rows, live_mask, chosen, rows_x, rows_y = gather_turn(first_row)
        colour, transmit = render(chosen, rows_x, rows_y, live_mask)
        packed = jnp.concatenate([colour, transmit[:, None, :]], axis=1)
        return lax.dynamic_update_slice_in_dim(partial_value, packed, first_row, 0)

    partial_value = lax.fori_loop(
        0, turn_count, forward_turn, jnp.broadcast_to(default, (slots_count, 4, pixels))
    )
    target = jnp.where(tile_ids >= 0, tile_ids // tiles_per, parts_count)
    tag_width = 128
    rows_out = jnp.concatenate(
        [
            partial_value.reshape(slots_count, 4 * pixels),
            jnp.broadcast_to(
                (tile_ids % tiles_per).astype(jnp.float32)[:, None], (slots_count, tag_width)
            ),
        ],
        axis=1,
    )
    route = (
        target[None, :] == jnp.arange(parts_count, dtype=jnp.int32)[:, None]
    ).astype(jnp.float32)
    unrouted = 1.0 - jnp.sum(route, axis=1)
    blank_row = jnp.concatenate(
        [default.reshape(4 * pixels), jnp.zeros((tag_width,), jnp.float32)], axis=0
    )
    payload = (
        jnp.einsum("ds,sz->dz", route, rows_out, precision=lax.Precision.HIGHEST)
        + unrouted[:, None] * blank_row[None, :]
    )
    landed = lax.all_to_all(payload, "dom", split_axis=0, concat_axis=0, tiled=True)
    second_here = landed[:, 4 * pixels] > 0.5
    landed = landed[:, : 4 * pixels].reshape(parts_count, 4, pixels)
    blank = jnp.broadcast_to(default, landed.shape)
    arrived = jnp.stack(
        [
            jnp.where(second_here[:, None, None], blank, landed),
            jnp.where(second_here[:, None, None], landed, blank),
        ],
        axis=1,
    )
    rendered, upstream = composite(arrived, orders, cotangent)
    sent_back = jnp.where(second_here[:, None, None], upstream[:, 1], upstream[:, 0])
    returned = lax.all_to_all(sent_back, "dom", split_axis=0, concat_axis=0, tiled=True)
    slot_grads = jnp.take(returned, jnp.maximum(tile_ids, 0) // tiles_per, axis=0)

    def backward_turn(turn_index, compact):
        first_row = turn_index * turn_rows
        index_rows, live_mask, chosen, rows_x, rows_y = gather_turn(first_row)
        upper_cot = lax.dynamic_slice_in_dim(slot_grads, first_row, turn_rows, 0)
        _, pullback = jax.vjp(lambda values: render(values, rows_x, rows_y, live_mask), chosen)
        grad_chosen = pullback((upper_cot[:, :3], upper_cot[:, 3]))[0]
        return lax.dynamic_update_slice_in_dim(compact, grad_chosen, first_row, 1)

    compact = lax.fori_loop(
        0, turn_count, backward_turn, jnp.zeros(chosen_all.shape, jnp.float32)
    )
    rows_count = params.shape[0]
    flat_index = jnp.where(live_all, entries, -1).reshape(-1)
    values = jnp.where(live_all[None], compact, 0.0).reshape(rows_count, -1)
    hi_index = jnp.where(flat_index >= 0, flat_index // lo_size, -1)
    lo_index = flat_index % lo_size
    spread = values[:, None, :] * (
        hi_index[None, None, :] == jnp.arange(hi_size, dtype=jnp.int32)[None, :, None]
    ).astype(jnp.float32)
    lo_hot = (lo_index[None, :] == jnp.arange(lo_size, dtype=jnp.int32)[:, None]).astype(
        jnp.float32
    )
    placed = jnp.einsum("che,le->chl", spread, lo_hot, precision=lax.Precision.HIGH)
    gathered = lax.all_to_all(placed, "tile", split_axis=1, concat_axis=1, tiled=True)
    total = jnp.sum(
        gathered.reshape(rows_count, groups_count, hi_size // groups_count, lo_size), axis=1
    )
    shares = total.reshape(rows_count, shard)
    return (rendered, shares[:5], shares[5], shares[6:])


def solution(mesh):
    placed = (
        P(None, "dom"),
        P("dom"),
        P(None, "dom"),
        P("dom", "tile", None),
        P("dom", "tile", None, None),
        P(("dom", "tile"), None),
        P(None, ("dom", "tile"), None),
    )
    return jax.shard_map(
        local,
        mesh=mesh,
        in_specs=placed,
        out_specs=(
            P(None, ("dom", "tile"), None),
            P(None, ("dom", "tile")),
            P(("dom", "tile")),
            P(None, ("dom", "tile")),
        ),
        check_vma=False,
    )
```

```python
import math

import jax
import jax.numpy as jnp
from jax import lax
from jax.sharding import PartitionSpec as P

TSIDE = 16


@jax.custom_vjp
def reuse_before(log_keep, saved):
    return saved


def reuse_before_fwd(log_keep, saved):
    return saved, None


def reuse_before_bwd(_, grad):
    entries_count = grad.shape[2]
    ahead = (
        jnp.arange(entries_count, dtype=jnp.int32)[:, None]
        < jnp.arange(entries_count, dtype=jnp.int32)[None, :]
    ).astype(jnp.float32)
    grad_keep = jnp.einsum("kph,gh->kpg", grad, ahead, precision=lax.Precision.HIGHEST)
    return (grad_keep, jnp.zeros_like(grad))


reuse_before.defvjp(reuse_before_fwd, reuse_before_bwd)


def render(params, pixel_x, pixel_y, live_mask, saved_before=None):
    centre_x = params[0][:, None, :]
    centre_y = params[1][:, None, :]
    inv_one = jnp.exp(-2.0 * params[2])
    inv_two = jnp.exp(-2.0 * params[3])
    cosine = jnp.cos(params[4])
    sine_angle = jnp.sin(params[4])
    coef_a = (cosine * cosine * inv_one + sine_angle * sine_angle * inv_two)[:, None, :]
    coef_b = (cosine * sine_angle * (inv_one - inv_two))[:, None, :]
    coef_c = (sine_angle * sine_angle * inv_one + cosine * cosine * inv_two)[:, None, :]
    delta_x = pixel_x[:, :, None] - centre_x
    delta_y = pixel_y[:, :, None] - centre_y
    quadratic = (
        coef_a * delta_x * delta_x + 2.0 * coef_b * delta_x * delta_y + coef_c * delta_y * delta_y
    )
    strength = jax.nn.sigmoid(params[5]) * live_mask
    opaque_part = strength[:, None, :] * jnp.exp(-0.5 * quadratic)
    log_keep = jnp.log1p(-opaque_part)
    entries_count = log_keep.shape[2]
    ahead = (
        jnp.arange(entries_count, dtype=jnp.int32)[:, None]
        < jnp.arange(entries_count, dtype=jnp.int32)[None, :]
    ).astype(jnp.float32)
    if saved_before is None:
        before = jnp.einsum("kpg,gh->kph", log_keep, ahead, precision=lax.Precision.HIGHEST)
    else:
        before = reuse_before(log_keep, saved_before)
    weight = opaque_part * jnp.exp(before)
    colour = jnp.einsum("kpg,ckg->kcp", weight, params[6:9], precision=lax.Precision.HIGHEST)
    transmit = jnp.exp(jnp.sum(log_keep, axis=2))
    return (colour, transmit, before)


def pixel_grid(tile_ids, group_index, tiles_per, pixels):
    safe_ids = jnp.maximum(tile_ids, 0)
    block_row = safe_ids // tiles_per
    column = group_index * tiles_per + safe_ids % tiles_per
    within = jnp.arange(pixels, dtype=jnp.int32)
    pixel_x = (column[:, None] * TSIDE + within[None, :] % TSIDE).astype(jnp.float32) + 0.5
    pixel_y = (block_row[:, None] * TSIDE + within[None, :] // TSIDE).astype(jnp.float32) + 0.5
    return (pixel_x, pixel_y)


def composite(arrived, orders, cotangent):
    parts_count = arrived.shape[0]
    ranks_onehot = (
        orders[:, None, :] == jnp.arange(parts_count, dtype=jnp.int32)[None, :, None]
    ).astype(jnp.float32)
    ordered = jnp.einsum("irk,kicp->ircp", ranks_onehot, arrived, precision=lax.Precision.HIGHEST)
    colour = ordered[:, :, :3]
    transmit = ordered[:, :, 3]
    ahead = (
        jnp.arange(parts_count, dtype=jnp.int32)[:, None]
        < jnp.arange(parts_count, dtype=jnp.int32)[None, :]
    ).astype(jnp.float32)
    prefix = jnp.exp(
        jnp.einsum("iqp,qr->irp", jnp.log(transmit), ahead, precision=lax.Precision.HIGHEST)
    )
    rendered = jnp.sum(prefix[:, :, None, :] * colour, axis=1)
    upstream_cot = jnp.transpose(cotangent, (1, 0, 2))
    grad_colour = prefix[:, :, None, :] * upstream_cot[:, None]
    weighted = prefix * jnp.sum(upstream_cot[:, None] * colour, axis=2)
    behind = jnp.einsum("iqp,rq->irp", weighted, ahead, precision=lax.Precision.HIGHEST)
    grad_transmit = behind / transmit
    grad_ordered = jnp.concatenate([grad_colour, grad_transmit[:, :, None, :]], axis=2)
    upstream = jnp.einsum(
        "irk,ircp->kicp", ranks_onehot, grad_ordered, precision=lax.Precision.HIGHEST
    )
    return (jnp.transpose(rendered, (1, 0, 2)), upstream)


def local(geometry, opacity, colours, coverage, gauss_lists, orders, cotangent):
    parts_count = lax.axis_size("dom")
    group_index = lax.axis_index("tile")
    tiles_per = orders.shape[0]
    pixels = cotangent.shape[2]
    params = jnp.concatenate([geometry, opacity[None, :], colours], axis=0)
    gauss_total = params.shape[1]
    tile_ids = coverage[0, 0]
    entries = gauss_lists[0, 0]
    slots_count = tile_ids.shape[0]
    turn_rows = math.gcd(slots_count, 4)
    covered = jnp.sum((tile_ids >= 0).astype(jnp.int32))
    turn_count = (covered + turn_rows - 1) // turn_rows
    pixel_x, pixel_y = pixel_grid(tile_ids, group_index, tiles_per, pixels)
    default = jnp.concatenate(
        [jnp.zeros((3, pixels), jnp.float32), jnp.ones((1, pixels), jnp.float32)], axis=0
    )

    live_all = entries >= 0
    groups_count = lax.axis_size("tile")
    shard = gauss_total // groups_count
    lo_size = 384 if shard % 384 == 0 else shard
    hi_size = gauss_total // lo_size
    safe_index = jnp.where(live_all, entries, 0).reshape(-1)
    hi_pick = (
        safe_index[None, None, :] // lo_size
        == jnp.arange(hi_size, dtype=jnp.int32)[:, None, None]
    ).astype(jnp.float32)
    lo_pick = (
        safe_index[None, :] % lo_size == jnp.arange(lo_size, dtype=jnp.int32)[:, None]
    ).astype(jnp.float32)
    by_row = jnp.einsum(
        "chl,le->hce",
        params.reshape(params.shape[0], hi_size, lo_size),
        lo_pick,
        precision=lax.Precision.HIGHEST,
    )
    chosen_all = jnp.sum(by_row * hi_pick, axis=0).reshape((params.shape[0],) + entries.shape)
    live_all_f = live_all.astype(jnp.float32)

    def gather_turn(first_row):
        index_rows = lax.dynamic_slice_in_dim(entries, first_row, turn_rows, 0)
        live = lax.dynamic_slice_in_dim(live_all_f, first_row, turn_rows, 0)
        chosen = lax.dynamic_slice_in_dim(chosen_all, first_row, turn_rows, 1)
        rows_x = lax.dynamic_slice_in_dim(pixel_x, first_row, turn_rows, 0)
        rows_y = lax.dynamic_slice_in_dim(pixel_y, first_row, turn_rows, 0)
        return (index_rows, live, chosen, rows_x, rows_y)

    def forward_turn(turn_index, carried):
        partial_value, saved = carried
        first_row = turn_index * turn_rows
        index_rows, live_mask, chosen, rows_x, rows_y = gather_turn(first_row)
        colour, transmit, before = render(chosen, rows_x, rows_y, live_mask)
        packed = jnp.concatenate([colour, transmit[:, None, :]], axis=1)
        return (
            lax.dynamic_update_slice_in_dim(partial_value, packed, first_row, 0),
            lax.dynamic_update_slice_in_dim(saved, before, first_row, 0),
        )

    partial_value, saved_all = lax.fori_loop(
        0,
        turn_count,
        forward_turn,
        (
            jnp.broadcast_to(default, (slots_count, 4, pixels)),
            jnp.zeros((slots_count, pixels, entries.shape[1]), jnp.float32),
        ),
    )
    target = jnp.where(tile_ids >= 0, tile_ids // tiles_per, parts_count)
    tag_width = 128
    rows_out = jnp.concatenate(
        [
            partial_value.reshape(slots_count, 4 * pixels),
            jnp.broadcast_to(
                (tile_ids % tiles_per).astype(jnp.float32)[:, None], (slots_count, tag_width)
            ),
        ],
        axis=1,
    )
    route = (
        target[None, :] == jnp.arange(parts_count, dtype=jnp.int32)[:, None]
    ).astype(jnp.float32)
    unrouted = 1.0 - jnp.sum(route, axis=1)
    blank_row = jnp.concatenate(
        [default.reshape(4 * pixels), jnp.zeros((tag_width,), jnp.float32)], axis=0
    )
    payload = (
        jnp.einsum("ds,sz->dz", route, rows_out, precision=lax.Precision.HIGHEST)
        + unrouted[:, None] * blank_row[None, :]
    )
    landed = lax.all_to_all(payload, "dom", split_axis=0, concat_axis=0, tiled=True)
    second_here = landed[:, 4 * pixels] > 0.5
    landed = landed[:, : 4 * pixels].reshape(parts_count, 4, pixels)
    blank = jnp.broadcast_to(default, landed.shape)
    arrived = jnp.stack(
        [
            jnp.where(second_here[:, None, None], blank, landed),
            jnp.where(second_here[:, None, None], landed, blank),
        ],
        axis=1,
    )
    rendered, upstream = composite(arrived, orders, cotangent)
    sent_back = jnp.where(second_here[:, None, None], upstream[:, 1], upstream[:, 0])
    returned = lax.all_to_all(sent_back, "dom", split_axis=0, concat_axis=0, tiled=True)
    slot_grads = jnp.take(returned, jnp.maximum(tile_ids, 0) // tiles_per, axis=0)

    def backward_turn(turn_index, compact):
        first_row = turn_index * turn_rows
        index_rows, live_mask, chosen, rows_x, rows_y = gather_turn(first_row)
        upper_cot = lax.dynamic_slice_in_dim(slot_grads, first_row, turn_rows, 0)
        saved = lax.dynamic_slice_in_dim(saved_all, first_row, turn_rows, 0)
        _, pullback = jax.vjp(
            lambda values: render(values, rows_x, rows_y, live_mask, saved)[:2], chosen
        )
        grad_chosen = pullback((upper_cot[:, :3], upper_cot[:, 3]))[0]
        return lax.dynamic_update_slice_in_dim(compact, grad_chosen, first_row, 1)

    compact = lax.fori_loop(
        0, turn_count, backward_turn, jnp.zeros(chosen_all.shape, jnp.float32)
    )
    rows_count = params.shape[0]
    flat_index = jnp.where(live_all, entries, -1).reshape(-1)
    values = jnp.where(live_all[None], compact, 0.0).reshape(rows_count, -1)
    hi_index = jnp.where(flat_index >= 0, flat_index // lo_size, -1)
    lo_index = flat_index % lo_size
    spread = values[:, None, :] * (
        hi_index[None, None, :] == jnp.arange(hi_size, dtype=jnp.int32)[None, :, None]
    ).astype(jnp.float32)
    lo_hot = (lo_index[None, :] == jnp.arange(lo_size, dtype=jnp.int32)[:, None]).astype(
        jnp.float32
    )
    placed = jnp.einsum("che,le->chl", spread, lo_hot, precision=lax.Precision.HIGH)
    gathered = lax.all_to_all(placed, "tile", split_axis=1, concat_axis=1, tiled=True)
    total = jnp.sum(
        gathered.reshape(rows_count, groups_count, hi_size // groups_count, lo_size), axis=1
    )
    shares = total.reshape(rows_count, shard)
    return (rendered, shares[:5], shares[5], shares[6:])


def solution(mesh):
    placed = (
        P(None, "dom"),
        P("dom"),
        P(None, "dom"),
        P("dom", "tile", None),
        P("dom", "tile", None, None),
        P(("dom", "tile"), None),
        P(None, ("dom", "tile"), None),
    )
    return jax.shard_map(
        local,
        mesh=mesh,
        in_specs=placed,
        out_specs=(
            P(None, ("dom", "tile"), None),
            P(None, ("dom", "tile")),
            P(("dom", "tile")),
            P(None, ("dom", "tile")),
        ),
        check_vma=False,
    )
```

```python
import math

import jax
import jax.numpy as jnp
from jax import lax
from jax.sharding import PartitionSpec as P

TSIDE = 16


def render(params, pixel_x, pixel_y, live_mask):
    centre_x = params[0][:, None, :]
    centre_y = params[1][:, None, :]
    inv_one = jnp.exp(-2.0 * params[2])
    inv_two = jnp.exp(-2.0 * params[3])
    cosine = jnp.cos(params[4])
    sine_angle = jnp.sin(params[4])
    coef_a = (cosine * cosine * inv_one + sine_angle * sine_angle * inv_two)[:, None, :]
    coef_b = (cosine * sine_angle * (inv_one - inv_two))[:, None, :]
    coef_c = (sine_angle * sine_angle * inv_one + cosine * cosine * inv_two)[:, None, :]
    delta_x = pixel_x[:, :, None] - centre_x
    delta_y = pixel_y[:, :, None] - centre_y
    quadratic = (
        coef_a * delta_x * delta_x + 2.0 * coef_b * delta_x * delta_y + coef_c * delta_y * delta_y
    )
    strength = jax.nn.sigmoid(params[5]) * live_mask
    opaque_part = strength[:, None, :] * jnp.exp(-0.5 * quadratic)
    log_keep = jnp.log1p(-opaque_part)
    entries_count = log_keep.shape[2]
    ahead = (
        jnp.arange(entries_count, dtype=jnp.int32)[:, None]
        < jnp.arange(entries_count, dtype=jnp.int32)[None, :]
    ).astype(jnp.float32)
    before = jnp.einsum("kpg,gh->kph", log_keep, ahead, precision=lax.Precision.HIGHEST)
    weight = opaque_part * jnp.exp(before)
    colour = jnp.einsum("kpg,ckg->kcp", weight, params[6:9], precision=lax.Precision.HIGHEST)
    transmit = jnp.exp(jnp.sum(log_keep, axis=2))
    return (colour, transmit)


def pixel_grid(tile_ids, group_index, tiles_per, pixels):
    safe_ids = jnp.maximum(tile_ids, 0)
    block_row = safe_ids // tiles_per
    column = group_index * tiles_per + safe_ids % tiles_per
    within = jnp.arange(pixels, dtype=jnp.int32)
    pixel_x = (column[:, None] * TSIDE + within[None, :] % TSIDE).astype(jnp.float32) + 0.5
    pixel_y = (block_row[:, None] * TSIDE + within[None, :] // TSIDE).astype(jnp.float32) + 0.5
    return (pixel_x, pixel_y)


def composite(arrived, orders, cotangent):
    parts_count = arrived.shape[0]
    ranks_onehot = (
        orders[:, None, :] == jnp.arange(parts_count, dtype=jnp.int32)[None, :, None]
    ).astype(jnp.float32)
    ordered = jnp.einsum("irk,kicp->ircp", ranks_onehot, arrived, precision=lax.Precision.HIGHEST)
    colour = ordered[:, :, :3]
    transmit = ordered[:, :, 3]
    ahead = (
        jnp.arange(parts_count, dtype=jnp.int32)[:, None]
        < jnp.arange(parts_count, dtype=jnp.int32)[None, :]
    ).astype(jnp.float32)
    prefix = jnp.exp(
        jnp.einsum("iqp,qr->irp", jnp.log(transmit), ahead, precision=lax.Precision.HIGHEST)
    )
    rendered = jnp.sum(prefix[:, :, None, :] * colour, axis=1)
    upstream_cot = jnp.transpose(cotangent, (1, 0, 2))
    grad_colour = prefix[:, :, None, :] * upstream_cot[:, None]
    weighted = prefix * jnp.sum(upstream_cot[:, None] * colour, axis=2)
    behind = jnp.einsum("iqp,rq->irp", weighted, ahead, precision=lax.Precision.HIGHEST)
    grad_transmit = behind / transmit
    grad_ordered = jnp.concatenate([grad_colour, grad_transmit[:, :, None, :]], axis=2)
    upstream = jnp.einsum(
        "irk,ircp->kicp", ranks_onehot, grad_ordered, precision=lax.Precision.HIGHEST
    )
    return (jnp.transpose(rendered, (1, 0, 2)), upstream)


def local(geometry, opacity, colours, coverage, gauss_lists, orders, cotangent):
    parts_count = lax.axis_size("dom")
    group_index = lax.axis_index("tile")
    tiles_per = orders.shape[0]
    pixels = cotangent.shape[2]
    params = jnp.concatenate([geometry, opacity[None, :], colours], axis=0)
    gauss_total = params.shape[1]
    tile_ids = coverage[0, 0]
    entries = gauss_lists[0, 0]
    slots_count = tile_ids.shape[0]
    turn_rows = math.gcd(slots_count, 4)
    covered = jnp.sum((tile_ids >= 0).astype(jnp.int32))
    turn_count = (covered + turn_rows - 1) // turn_rows
    pixel_x, pixel_y = pixel_grid(tile_ids, group_index, tiles_per, pixels)
    default = jnp.concatenate(
        [jnp.zeros((3, pixels), jnp.float32), jnp.ones((1, pixels), jnp.float32)], axis=0
    )

    live_all = entries >= 0
    groups_count = lax.axis_size("tile")
    shard = gauss_total // groups_count
    lo_size = 384 if shard % 384 == 0 else shard
    hi_size = gauss_total // lo_size
    safe_index = jnp.where(live_all, entries, 0).reshape(-1)
    hi_pick = (
        safe_index[None, None, :] // lo_size
        == jnp.arange(hi_size, dtype=jnp.int32)[:, None, None]
    ).astype(jnp.float32)
    lo_pick = (
        safe_index[None, :] % lo_size == jnp.arange(lo_size, dtype=jnp.int32)[:, None]
    ).astype(jnp.float32)
    by_row = jnp.einsum(
        "chl,le->hce",
        params.reshape(params.shape[0], hi_size, lo_size),
        lo_pick,
        precision=lax.Precision.HIGHEST,
    )
    chosen_all = jnp.sum(by_row * hi_pick, axis=0).reshape((params.shape[0],) + entries.shape)
    live_all_f = live_all.astype(jnp.float32)

    def gather_turn(first_row):
        index_rows = lax.dynamic_slice_in_dim(entries, first_row, turn_rows, 0)
        live = lax.dynamic_slice_in_dim(live_all_f, first_row, turn_rows, 0)
        chosen = lax.dynamic_slice_in_dim(chosen_all, first_row, turn_rows, 1)
        rows_x = lax.dynamic_slice_in_dim(pixel_x, first_row, turn_rows, 0)
        rows_y = lax.dynamic_slice_in_dim(pixel_y, first_row, turn_rows, 0)
        return (index_rows, live, chosen, rows_x, rows_y)

    def forward_turn(turn_index, partial_value):
        first_row = turn_index * turn_rows
        index_rows, live_mask, chosen, rows_x, rows_y = gather_turn(first_row)
        colour, transmit = render(chosen, rows_x, rows_y, live_mask)
        packed = jnp.concatenate([colour, transmit[:, None, :]], axis=1)
        return lax.dynamic_update_slice_in_dim(partial_value, packed, first_row, 0)

    partial_value = lax.fori_loop(
        0, turn_count, forward_turn, jnp.broadcast_to(default, (slots_count, 4, pixels))
    )
    target = jnp.where(tile_ids >= 0, tile_ids // tiles_per, parts_count)
    tag_width = 128
    rows_out = jnp.concatenate(
        [
            partial_value.reshape(slots_count, 4 * pixels),
            jnp.broadcast_to(
                (tile_ids % tiles_per).astype(jnp.float32)[:, None], (slots_count, tag_width)
            ),
        ],
        axis=1,
    )
    route = (
        target[None, :] == jnp.arange(parts_count, dtype=jnp.int32)[:, None]
    ).astype(jnp.float32)
    unrouted = 1.0 - jnp.sum(route, axis=1)
    blank_row = jnp.concatenate(
        [default.reshape(4 * pixels), jnp.zeros((tag_width,), jnp.float32)], axis=0
    )
    payload = (
        jnp.einsum("ds,sz->dz", route, rows_out, precision=lax.Precision.HIGHEST)
        + unrouted[:, None] * blank_row[None, :]
    )
    landed = lax.all_to_all(payload, "dom", split_axis=0, concat_axis=0, tiled=True)
    second_here = landed[:, 4 * pixels] > 0.5
    landed = landed[:, : 4 * pixels].reshape(parts_count, 4, pixels)
    blank = jnp.broadcast_to(default, landed.shape)
    arrived = jnp.stack(
        [
            jnp.where(second_here[:, None, None], blank, landed),
            jnp.where(second_here[:, None, None], landed, blank),
        ],
        axis=1,
    )
    rendered, upstream = composite(arrived, orders, cotangent)
    sent_back = jnp.where(second_here[:, None, None], upstream[:, 1], upstream[:, 0])
    returned = lax.all_to_all(sent_back, "dom", split_axis=0, concat_axis=0, tiled=True)
    slot_grads = jnp.take(returned, jnp.maximum(tile_ids, 0) // tiles_per, axis=0)

    def backward_turn(turn_index, compact):
        first_row = turn_index * turn_rows
        index_rows, live_mask, chosen, rows_x, rows_y = gather_turn(first_row)
        upper_cot = lax.dynamic_slice_in_dim(slot_grads, first_row, turn_rows, 0)
        _, pullback = jax.vjp(lambda values: render(values, rows_x, rows_y, live_mask), chosen)
        grad_chosen = pullback((upper_cot[:, :3], upper_cot[:, 3]))[0]
        return lax.dynamic_update_slice_in_dim(compact, grad_chosen, first_row, 1)

    compact = lax.fori_loop(
        0, turn_count, backward_turn, jnp.zeros(chosen_all.shape, jnp.float32)
    )
    rows_count = params.shape[0]
    flat_index = jnp.where(live_all, entries, -1).reshape(-1)
    values = jnp.where(live_all[None], compact, 0.0).reshape(rows_count, -1)
    hi_index = jnp.where(flat_index >= 0, flat_index // lo_size, -1)
    lo_index = flat_index % lo_size
    spread = values[:, None, :] * (
        hi_index[None, None, :] == jnp.arange(hi_size, dtype=jnp.int32)[None, :, None]
    ).astype(jnp.float32)
    lo_hot = (lo_index[None, :] == jnp.arange(lo_size, dtype=jnp.int32)[:, None]).astype(
        jnp.float32
    )
    placed = jnp.einsum("che,le->chl", spread, lo_hot, precision=lax.Precision.HIGH)
    gathered = lax.all_to_all(placed, "tile", split_axis=1, concat_axis=1, tiled=True)
    arrived_grads = gathered.reshape(rows_count, groups_count, hi_size // groups_count, lo_size)

    def share_of(first, last):
        return jnp.sum(arrived_grads[first:last], axis=1).reshape(last - first, shard)

    return (rendered, share_of(0, 5), share_of(5, 6)[0], share_of(6, rows_count))


def solution(mesh):
    placed = (
        P(None, "dom"),
        P("dom"),
        P(None, "dom"),
        P("dom", "tile", None),
        P("dom", "tile", None, None),
        P(("dom", "tile"), None),
        P(None, ("dom", "tile"), None),
    )
    return jax.shard_map(
        local,
        mesh=mesh,
        in_specs=placed,
        out_specs=(
            P(None, ("dom", "tile"), None),
            P(None, ("dom", "tile")),
            P(("dom", "tile")),
            P(None, ("dom", "tile")),
        ),
        check_vma=False,
    )
```

```python
import math

import jax
import jax.numpy as jnp
from jax import lax
from jax.sharding import PartitionSpec as P

TSIDE = 16


def render(params, pixel_x, pixel_y, live_mask):
    centre_x = params[0][:, None, :]
    centre_y = params[1][:, None, :]
    inv_one = jnp.exp(-2.0 * params[2])
    inv_two = jnp.exp(-2.0 * params[3])
    cosine = jnp.cos(params[4])
    sine_angle = jnp.sin(params[4])
    coef_a = (cosine * cosine * inv_one + sine_angle * sine_angle * inv_two)[:, None, :]
    coef_b = (cosine * sine_angle * (inv_one - inv_two))[:, None, :]
    coef_c = (sine_angle * sine_angle * inv_one + cosine * cosine * inv_two)[:, None, :]
    delta_x = pixel_x[:, :, None] - centre_x
    delta_y = pixel_y[:, :, None] - centre_y
    quadratic = (
        coef_a * delta_x * delta_x + 2.0 * coef_b * delta_x * delta_y + coef_c * delta_y * delta_y
    )
    strength = jax.nn.sigmoid(params[5]) * live_mask
    opaque_part = strength[:, None, :] * jnp.exp(-0.5 * quadratic)
    log_keep = jnp.log1p(-opaque_part)
    entries_count = log_keep.shape[2]
    ahead = (
        jnp.arange(entries_count, dtype=jnp.int32)[:, None]
        < jnp.arange(entries_count, dtype=jnp.int32)[None, :]
    ).astype(jnp.float32)
    before = jnp.einsum("kpg,gh->kph", log_keep, ahead, precision=lax.Precision.HIGHEST)
    weight = opaque_part * jnp.exp(before)
    colour = jnp.einsum("kpg,ckg->kcp", weight, params[6:9], precision=lax.Precision.HIGHEST)
    transmit = jnp.exp(jnp.sum(log_keep, axis=2))
    return (colour, transmit)


def pixel_grid(tile_ids, group_index, tiles_per, pixels):
    safe_ids = jnp.maximum(tile_ids, 0)
    block_row = safe_ids // tiles_per
    column = group_index * tiles_per + safe_ids % tiles_per
    within = jnp.arange(pixels, dtype=jnp.int32)
    pixel_x = (column[:, None] * TSIDE + within[None, :] % TSIDE).astype(jnp.float32) + 0.5
    pixel_y = (block_row[:, None] * TSIDE + within[None, :] // TSIDE).astype(jnp.float32) + 0.5
    return (pixel_x, pixel_y)


def composite(arrived, orders, cotangent):
    parts_count = arrived.shape[0]
    ranks_onehot = (
        orders[:, None, :] == jnp.arange(parts_count, dtype=jnp.int32)[None, :, None]
    ).astype(jnp.float32)
    ordered = jnp.einsum("irk,kicp->ircp", ranks_onehot, arrived, precision=lax.Precision.HIGHEST)
    colour = ordered[:, :, :3]
    transmit = ordered[:, :, 3]
    ahead = (
        jnp.arange(parts_count, dtype=jnp.int32)[:, None]
        < jnp.arange(parts_count, dtype=jnp.int32)[None, :]
    ).astype(jnp.float32)
    prefix = jnp.exp(
        jnp.einsum("iqp,qr->irp", jnp.log(transmit), ahead, precision=lax.Precision.HIGHEST)
    )
    rendered = jnp.sum(prefix[:, :, None, :] * colour, axis=1)
    upstream_cot = jnp.transpose(cotangent, (1, 0, 2))
    grad_colour = prefix[:, :, None, :] * upstream_cot[:, None]
    weighted = prefix * jnp.sum(upstream_cot[:, None] * colour, axis=2)
    behind = jnp.einsum("iqp,rq->irp", weighted, ahead, precision=lax.Precision.HIGHEST)
    grad_transmit = behind / transmit
    grad_ordered = jnp.concatenate([grad_colour, grad_transmit[:, :, None, :]], axis=2)
    upstream = jnp.einsum(
        "irk,ircp->kicp", ranks_onehot, grad_ordered, precision=lax.Precision.HIGHEST
    )
    return (jnp.transpose(rendered, (1, 0, 2)), upstream)


def local(geometry, opacity, colours, coverage, gauss_lists, orders, cotangent):
    parts_count = lax.axis_size("dom")
    group_index = lax.axis_index("tile")
    tiles_per = orders.shape[0]
    pixels = cotangent.shape[2]
    params = jnp.concatenate([geometry, opacity[None, :], colours], axis=0)
    gauss_total = params.shape[1]
    tile_ids = coverage[0, 0]
    entries = gauss_lists[0, 0]
    slots_count = tile_ids.shape[0]
    turn_rows = math.gcd(slots_count, 4)
    covered = jnp.sum((tile_ids >= 0).astype(jnp.int32))
    turn_count = (covered + turn_rows - 1) // turn_rows
    pixel_x, pixel_y = pixel_grid(tile_ids, group_index, tiles_per, pixels)
    default = jnp.concatenate(
        [jnp.zeros((3, pixels), jnp.float32), jnp.ones((1, pixels), jnp.float32)], axis=0
    )

    live_all = entries >= 0
    groups_count = lax.axis_size("tile")
    shard = gauss_total // groups_count
    lo_size = 384 if shard % 384 == 0 else shard
    hi_size = gauss_total // lo_size
    safe_index = jnp.where(live_all, entries, 0).reshape(-1)
    hi_pick = (
        safe_index[None, None, :] // lo_size
        == jnp.arange(hi_size, dtype=jnp.int32)[:, None, None]
    ).astype(jnp.float32)
    lo_pick = (
        safe_index[None, :] % lo_size == jnp.arange(lo_size, dtype=jnp.int32)[:, None]
    ).astype(jnp.float32)
    by_row = jnp.einsum(
        "chl,le->hce",
        params.reshape(params.shape[0], hi_size, lo_size),
        lo_pick,
        precision=lax.Precision.HIGHEST,
    )
    chosen_all = jnp.sum(by_row * hi_pick, axis=0).reshape((params.shape[0],) + entries.shape)
    live_all_f = live_all.astype(jnp.float32)

    def gather_turn(first_row):
        index_rows = lax.dynamic_slice_in_dim(entries, first_row, turn_rows, 0)
        live = lax.dynamic_slice_in_dim(live_all_f, first_row, turn_rows, 0)
        chosen = lax.dynamic_slice_in_dim(chosen_all, first_row, turn_rows, 1)
        rows_x = lax.dynamic_slice_in_dim(pixel_x, first_row, turn_rows, 0)
        rows_y = lax.dynamic_slice_in_dim(pixel_y, first_row, turn_rows, 0)
        return (index_rows, live, chosen, rows_x, rows_y)

    def forward_turn(turn_index, partial_value):
        first_row = turn_index * turn_rows
        index_rows, live_mask, chosen, rows_x, rows_y = gather_turn(first_row)
        colour, transmit = render(chosen, rows_x, rows_y, live_mask)
        packed = jnp.concatenate([colour, transmit[:, None, :]], axis=1)
        return lax.dynamic_update_slice_in_dim(partial_value, packed, first_row, 0)

    partial_value = lax.fori_loop(
        0, turn_count, forward_turn, jnp.broadcast_to(default, (slots_count, 4, pixels))
    )
    target = jnp.where(tile_ids >= 0, tile_ids // tiles_per, parts_count)
    tag_width = 128
    rows_out = jnp.concatenate(
        [
            partial_value.reshape(slots_count, 4 * pixels),
            jnp.broadcast_to(
                (tile_ids % tiles_per).astype(jnp.float32)[:, None], (slots_count, tag_width)
            ),
        ],
        axis=1,
    )
    route = (
        target[None, :] == jnp.arange(parts_count, dtype=jnp.int32)[:, None]
    ).astype(jnp.float32)
    unrouted = 1.0 - jnp.sum(route, axis=1)
    blank_row = jnp.concatenate(
        [default.reshape(4 * pixels), jnp.zeros((tag_width,), jnp.float32)], axis=0
    )
    payload = (
        jnp.einsum("ds,sz->dz", route, rows_out, precision=lax.Precision.HIGHEST)
        + unrouted[:, None] * blank_row[None, :]
    )
    landed = lax.all_to_all(payload, "dom", split_axis=0, concat_axis=0, tiled=True)
    second_here = landed[:, 4 * pixels] > 0.5
    landed = landed[:, : 4 * pixels].reshape(parts_count, 4, pixels)
    blank = jnp.broadcast_to(default, landed.shape)
    arrived = jnp.stack(
        [
            jnp.where(second_here[:, None, None], blank, landed),
            jnp.where(second_here[:, None, None], landed, blank),
        ],
        axis=1,
    )
    rendered, upstream = composite(arrived, orders, cotangent)
    sent_back = jnp.where(second_here[:, None, None], upstream[:, 1], upstream[:, 0])
    returned = lax.all_to_all(sent_back, "dom", split_axis=0, concat_axis=0, tiled=True)
    slot_grads = jnp.einsum(
        "ds,dz->sz",
        route,
        returned.reshape(parts_count, 4 * pixels),
        precision=lax.Precision.HIGHEST,
    ).reshape(slots_count, 4, pixels)

    def backward_turn(turn_index, compact):
        first_row = turn_index * turn_rows
        index_rows, live_mask, chosen, rows_x, rows_y = gather_turn(first_row)
        upper_cot = lax.dynamic_slice_in_dim(slot_grads, first_row, turn_rows, 0)
        _, pullback = jax.vjp(lambda values: render(values, rows_x, rows_y, live_mask), chosen)
        grad_chosen = pullback((upper_cot[:, :3], upper_cot[:, 3]))[0]
        return lax.dynamic_update_slice_in_dim(compact, grad_chosen, first_row, 1)

    compact = lax.fori_loop(
        0, turn_count, backward_turn, jnp.zeros(chosen_all.shape, jnp.float32)
    )
    rows_count = params.shape[0]
    flat_index = jnp.where(live_all, entries, -1).reshape(-1)
    values = jnp.where(live_all[None], compact, 0.0).reshape(rows_count, -1)
    hi_index = jnp.where(flat_index >= 0, flat_index // lo_size, -1)
    lo_index = flat_index % lo_size
    spread = values[:, None, :] * (
        hi_index[None, None, :] == jnp.arange(hi_size, dtype=jnp.int32)[None, :, None]
    ).astype(jnp.float32)
    lo_hot = (lo_index[None, :] == jnp.arange(lo_size, dtype=jnp.int32)[:, None]).astype(
        jnp.float32
    )
    placed = jnp.einsum("che,le->chl", spread, lo_hot, precision=lax.Precision.HIGH)
    gathered = lax.all_to_all(placed, "tile", split_axis=1, concat_axis=1, tiled=True)
    arrived_grads = gathered.reshape(rows_count, groups_count, hi_size // groups_count, lo_size)

    def share_of(first, last):
        return jnp.sum(arrived_grads[first:last], axis=1).reshape(last - first, shard)

    return (rendered, share_of(0, 5), share_of(5, 6)[0], share_of(6, rows_count))


def solution(mesh):
    placed = (
        P(None, "dom"),
        P("dom"),
        P(None, "dom"),
        P("dom", "tile", None),
        P("dom", "tile", None, None),
        P(("dom", "tile"), None),
        P(None, ("dom", "tile"), None),
    )
    return jax.shard_map(
        local,
        mesh=mesh,
        in_specs=placed,
        out_specs=(
            P(None, ("dom", "tile"), None),
            P(None, ("dom", "tile")),
            P(("dom", "tile")),
            P(None, ("dom", "tile")),
        ),
        check_vma=False,
    )
```

```python
import math

import jax
import jax.numpy as jnp
from jax import lax
from jax.sharding import PartitionSpec as P

TSIDE = 16


def render(params, pixel_x, pixel_y, live_mask):
    centre_x = params[0][:, None, :]
    centre_y = params[1][:, None, :]
    inv_one = jnp.exp(-2.0 * params[2])
    inv_two = jnp.exp(-2.0 * params[3])
    cosine = jnp.cos(params[4])
    sine_angle = jnp.sin(params[4])
    coef_a = (cosine * cosine * inv_one + sine_angle * sine_angle * inv_two)[:, None, :]
    coef_b = (cosine * sine_angle * (inv_one - inv_two))[:, None, :]
    coef_c = (sine_angle * sine_angle * inv_one + cosine * cosine * inv_two)[:, None, :]
    delta_x = pixel_x[:, :, None] - centre_x
    delta_y = pixel_y[:, :, None] - centre_y
    quadratic = (
        coef_a * delta_x * delta_x + 2.0 * coef_b * delta_x * delta_y + coef_c * delta_y * delta_y
    )
    strength = jax.nn.sigmoid(params[5]) * live_mask
    opaque_part = strength[:, None, :] * jnp.exp(-0.5 * quadratic)
    log_keep = jnp.log1p(-opaque_part)
    entries_count = log_keep.shape[2]
    ahead = (
        jnp.arange(entries_count, dtype=jnp.int32)[:, None]
        < jnp.arange(entries_count, dtype=jnp.int32)[None, :]
    ).astype(jnp.float32)
    before = jnp.einsum("kpg,gh->kph", log_keep, ahead, precision=lax.Precision.HIGHEST)
    weight = opaque_part * jnp.exp(before)
    colour = jnp.einsum("kpg,ckg->kcp", weight, params[6:9], precision=lax.Precision.HIGHEST)
    transmit = jnp.exp(jnp.sum(log_keep, axis=2))
    return (colour, transmit)


def pixel_grid(tile_ids, group_index, tiles_per, pixels):
    safe_ids = jnp.maximum(tile_ids, 0)
    block_row = safe_ids // tiles_per
    column = group_index * tiles_per + safe_ids % tiles_per
    within = jnp.arange(pixels, dtype=jnp.int32)
    pixel_x = (column[:, None] * TSIDE + within[None, :] % TSIDE).astype(jnp.float32) + 0.5
    pixel_y = (block_row[:, None] * TSIDE + within[None, :] // TSIDE).astype(jnp.float32) + 0.5
    return (pixel_x, pixel_y)


def composite(arrived, orders, cotangent):
    parts_count = arrived.shape[0]
    ranks_onehot = (
        orders[:, None, :] == jnp.arange(parts_count, dtype=jnp.int32)[None, :, None]
    ).astype(jnp.float32)
    ordered = jnp.einsum("irk,kicp->ircp", ranks_onehot, arrived, precision=lax.Precision.HIGHEST)
    colour = ordered[:, :, :3]
    transmit = ordered[:, :, 3]
    ahead = (
        jnp.arange(parts_count, dtype=jnp.int32)[:, None]
        < jnp.arange(parts_count, dtype=jnp.int32)[None, :]
    ).astype(jnp.float32)
    prefix = jnp.exp(
        jnp.einsum("iqp,qr->irp", jnp.log(transmit), ahead, precision=lax.Precision.HIGHEST)
    )
    rendered = jnp.sum(prefix[:, :, None, :] * colour, axis=1)
    upstream_cot = jnp.transpose(cotangent, (1, 0, 2))
    grad_colour = prefix[:, :, None, :] * upstream_cot[:, None]
    weighted = prefix * jnp.sum(upstream_cot[:, None] * colour, axis=2)
    behind = jnp.einsum("iqp,rq->irp", weighted, ahead, precision=lax.Precision.HIGHEST)
    grad_transmit = behind / transmit
    grad_ordered = jnp.concatenate([grad_colour, grad_transmit[:, :, None, :]], axis=2)
    upstream = jnp.einsum(
        "irk,ircp->kicp", ranks_onehot, grad_ordered, precision=lax.Precision.HIGH
    )
    return (jnp.transpose(rendered, (1, 0, 2)), upstream)


def local(geometry, opacity, colours, coverage, gauss_lists, orders, cotangent):
    parts_count = lax.axis_size("dom")
    group_index = lax.axis_index("tile")
    tiles_per = orders.shape[0]
    pixels = cotangent.shape[2]
    params = jnp.concatenate([geometry, opacity[None, :], colours], axis=0)
    gauss_total = params.shape[1]
    tile_ids = coverage[0, 0]
    entries = gauss_lists[0, 0]
    slots_count = tile_ids.shape[0]
    turn_rows = math.gcd(slots_count, 4)
    covered = jnp.sum((tile_ids >= 0).astype(jnp.int32))
    turn_count = (covered + turn_rows - 1) // turn_rows
    pixel_x, pixel_y = pixel_grid(tile_ids, group_index, tiles_per, pixels)
    default = jnp.concatenate(
        [jnp.zeros((3, pixels), jnp.float32), jnp.ones((1, pixels), jnp.float32)], axis=0
    )

    live_all = entries >= 0
    groups_count = lax.axis_size("tile")
    shard = gauss_total // groups_count
    lo_size = 384 if shard % 384 == 0 else shard
    hi_size = gauss_total // lo_size
    safe_index = jnp.where(live_all, entries, 0).reshape(-1)
    hi_pick = (
        safe_index[None, None, :] // lo_size
        == jnp.arange(hi_size, dtype=jnp.int32)[:, None, None]
    ).astype(jnp.float32)
    lo_pick = (
        safe_index[None, :] % lo_size == jnp.arange(lo_size, dtype=jnp.int32)[:, None]
    ).astype(jnp.float32)
    by_row = jnp.einsum(
        "chl,le->hce",
        params.reshape(params.shape[0], hi_size, lo_size),
        lo_pick,
        precision=lax.Precision.HIGHEST,
    )
    chosen_all = jnp.sum(by_row * hi_pick, axis=0).reshape((params.shape[0],) + entries.shape)
    live_all_f = live_all.astype(jnp.float32)

    def gather_turn(first_row):
        index_rows = lax.dynamic_slice_in_dim(entries, first_row, turn_rows, 0)
        live = lax.dynamic_slice_in_dim(live_all_f, first_row, turn_rows, 0)
        chosen = lax.dynamic_slice_in_dim(chosen_all, first_row, turn_rows, 1)
        rows_x = lax.dynamic_slice_in_dim(pixel_x, first_row, turn_rows, 0)
        rows_y = lax.dynamic_slice_in_dim(pixel_y, first_row, turn_rows, 0)
        return (index_rows, live, chosen, rows_x, rows_y)

    def forward_turn(turn_index, partial_value):
        first_row = turn_index * turn_rows
        index_rows, live_mask, chosen, rows_x, rows_y = gather_turn(first_row)
        colour, transmit = render(chosen, rows_x, rows_y, live_mask)
        packed = jnp.concatenate([colour, transmit[:, None, :]], axis=1)
        return lax.dynamic_update_slice_in_dim(partial_value, packed, first_row, 0)

    partial_value = lax.fori_loop(
        0, turn_count, forward_turn, jnp.broadcast_to(default, (slots_count, 4, pixels))
    )
    target = jnp.where(tile_ids >= 0, tile_ids // tiles_per, parts_count)
    tag_width = 128
    rows_out = jnp.concatenate(
        [
            partial_value.reshape(slots_count, 4 * pixels),
            jnp.broadcast_to(
                (tile_ids % tiles_per).astype(jnp.float32)[:, None], (slots_count, tag_width)
            ),
        ],
        axis=1,
    )
    route = (
        target[None, :] == jnp.arange(parts_count, dtype=jnp.int32)[:, None]
    ).astype(jnp.float32)
    unrouted = 1.0 - jnp.sum(route, axis=1)
    blank_row = jnp.concatenate(
        [default.reshape(4 * pixels), jnp.zeros((tag_width,), jnp.float32)], axis=0
    )
    payload = (
        jnp.einsum("ds,sz->dz", route, rows_out, precision=lax.Precision.HIGHEST)
        + unrouted[:, None] * blank_row[None, :]
    )
    landed = lax.all_to_all(payload, "dom", split_axis=0, concat_axis=0, tiled=True)
    second_here = landed[:, 4 * pixels] > 0.5
    landed = landed[:, : 4 * pixels].reshape(parts_count, 4, pixels)
    blank = jnp.broadcast_to(default, landed.shape)
    arrived = jnp.stack(
        [
            jnp.where(second_here[:, None, None], blank, landed),
            jnp.where(second_here[:, None, None], landed, blank),
        ],
        axis=1,
    )
    rendered, upstream = composite(arrived, orders, cotangent)
    sent_back = jnp.where(second_here[:, None, None], upstream[:, 1], upstream[:, 0])
    returned = lax.all_to_all(sent_back, "dom", split_axis=0, concat_axis=0, tiled=True)
    slot_grads = jnp.einsum(
        "ds,dz->sz",
        route,
        returned.reshape(parts_count, 4 * pixels),
        precision=lax.Precision.HIGHEST,
    ).reshape(slots_count, 4, pixels)

    def backward_turn(turn_index, compact):
        first_row = turn_index * turn_rows
        index_rows, live_mask, chosen, rows_x, rows_y = gather_turn(first_row)
        upper_cot = lax.dynamic_slice_in_dim(slot_grads, first_row, turn_rows, 0)
        _, pullback = jax.vjp(lambda values: render(values, rows_x, rows_y, live_mask), chosen)
        grad_chosen = pullback((upper_cot[:, :3], upper_cot[:, 3]))[0]
        return lax.dynamic_update_slice_in_dim(compact, grad_chosen, first_row, 1)

    compact = lax.fori_loop(
        0, turn_count, backward_turn, jnp.zeros(chosen_all.shape, jnp.float32)
    )
    rows_count = params.shape[0]
    flat_index = jnp.where(live_all, entries, -1).reshape(-1)
    values = jnp.where(live_all[None], compact, 0.0).reshape(rows_count, -1)
    hi_index = jnp.where(flat_index >= 0, flat_index // lo_size, -1)
    lo_index = flat_index % lo_size
    spread = values[:, None, :] * (
        hi_index[None, None, :] == jnp.arange(hi_size, dtype=jnp.int32)[None, :, None]
    ).astype(jnp.float32)
    lo_hot = (lo_index[None, :] == jnp.arange(lo_size, dtype=jnp.int32)[:, None]).astype(
        jnp.float32
    )
    placed = jnp.einsum("che,le->chl", spread, lo_hot, precision=lax.Precision.HIGH)
    gathered = lax.all_to_all(placed, "tile", split_axis=1, concat_axis=1, tiled=True)
    arrived_grads = gathered.reshape(rows_count, groups_count, hi_size // groups_count, lo_size)

    def share_of(first, last):
        return jnp.sum(arrived_grads[first:last], axis=1).reshape(last - first, shard)

    return (rendered, share_of(0, 5), share_of(5, 6)[0], share_of(6, rows_count))


def solution(mesh):
    placed = (
        P(None, "dom"),
        P("dom"),
        P(None, "dom"),
        P("dom", "tile", None),
        P("dom", "tile", None, None),
        P(("dom", "tile"), None),
        P(None, ("dom", "tile"), None),
    )
    return jax.shard_map(
        local,
        mesh=mesh,
        in_specs=placed,
        out_specs=(
            P(None, ("dom", "tile"), None),
            P(None, ("dom", "tile")),
            P(("dom", "tile")),
            P(None, ("dom", "tile")),
        ),
        check_vma=False,
    )
```
